128 devices in a mesh: req: 16 (over x, y), kv: 8 (over z, core).
Axes of the slice: x: 4, y: 4, z: 4, core: 2. Of those that a mesh axis runs over, the one named last changes fastest.
Arguments:
- hidden: bfloat16 [1024, 2048], P('req', 'kv'), may hold values from -6 to 6
- attn_gain: float32 [2048], replicated, may hold values from 0.25 to 1.75
- q_gain: float32 [128], replicated, may hold values from 0.25 to 1.75
- k_gain: float32 [128], replicated, may hold values from 0.25 to 1.75
- w_q: bfloat16 [2048, 2048], P(None, 'kv'), may hold values from -0.125 to 0.125
- w_gate_attn: bfloat16 [2048, 2048], P(None, 'kv'), may hold values from -0.125 to 0.125
- w_k: bfloat16 [2048, 1024], P(None, 'kv'), may hold values from -0.125 to 0.125
- w_v: bfloat16 [2048, 1024], P(None, 'kv'), may hold values from -0.125 to 0.125
- w_o: bfloat16 [2048, 2048], P('kv'), may hold values from -0.125 to 0.125
- k_pool: bfloat16 [2784, 128, 1024], P('req', None, 'kv'), may hold values from -245 to 245
- v_pool: bfloat16 [2784, 128, 1024], P('req', None, 'kv'), may hold values from -6 to 6
- lengths: int32 [1024], P('req'), may hold values from 1 to 4095, as said below
- page_table: int32 [1024, 32], P('req'), may hold values from 0 to 173, as said below
- mig_request: int32 [16, 16], P('req'), may hold values from 0 to 63, as said below
- mig_dest: int32 [16, 16], P('req'), may hold values from 0 to 15, as said below
- mlp_gain: float32 [2048], replicated, may hold values from 0.25 to 1.75
- w_gate: bfloat16 [2048, 6144], P(None, ('req', 'kv')), may hold values from -0.125 to 0.125
- w_up: bfloat16 [2048, 6144], P(None, ('req', 'kv')), may hold values from -0.125 to 0.125
- w_down: bfloat16 [2048, 6144], P(None, ('req', 'kv')), may hold values from -0.078125 to 0.078125
Outputs:
- out_hidden: bfloat16 [1024, 2048], P('req', 'kv')
- mig_keys: bfloat16 [256, 512, 1024], P('req', None, 'kv')
- mig_values: bfloat16 [256, 512, 1024], P('req', None, 'kv')
The draws below stay inside these ranges and needn't reach their ends.
Inputs may be any that keep to these rules, and one draw needn't show every extreme that they name: lengths[r] tokens of request r are cached and its new token takes position lengths[r]; some request holds 4095 cached tokens. `page_table`: entries refer to the pool of the request's own device. The first lengths[r] // 128 + 1 entries of row r are the request's pages, distinct and never shared with another request of that device; later entries are valid pages that are not read. `mig_request`: row s names 16 different requests of device s; each has at most 511 cached tokens, and in every row one has exactly that many. `mig_dest`: each row is a permutation.
All inputs are finite; a program needn't handle non-finite values.
Results may differ from the reference program's by a relative error of at most 0.0093.
Values may be sent and summed in bfloat16 or wider, within the bound.
No kernel may reach another device: no remote copies, remote signals or barrier semaphores. Data moves between devices by JAX's collectives and lax.ppermute only.
A program may use at most 128 MiB of HBM per device.

```python
import jax
import jax.numpy as jnp
from jax import lax

D = 2048
H = 16
KVH = 8
HD = 128
FF = 6144
R_DEV = 64
PAGE = 128
MAXP = 32
MIGP = 4
REQS = 1024
POOL_DEV = 174
N_REQ = 16


def permute_rows(key, row_number, length):
    split_keys = jax.random.split(key, row_number)

    def one_row(row_key):
        return jax.random.permutation(row_key, length)
    return jax.vmap(one_row)(split_keys)


def layout(key):
    heavy_total = max(1, N_REQ // 8)
    dev_order = jax.random.permutation(jax.random.fold_in(key, 11), N_REQ)
    heavy_dev = (dev_order < heavy_total)[:, None]
    local_rank = permute_rows(jax.random.fold_in(key, 12), N_REQ, R_DEV)
    migrant = local_rank < N_REQ
    long_one = heavy_dev & (local_rank >= N_REQ) & (local_rank < N_REQ + 2)
    mid_pages = jax.random.randint(jax.random.fold_in(key, 13), (N_REQ, R_DEV), 2, MIGP + 1)
    page_count = jnp.where(migrant, jnp.where(local_rank == 0, MIGP, mid_pages), jnp.where(long_one, MAXP, 1))
    spread = jax.random.randint(jax.random.fold_in(key, 14), (N_REQ, R_DEV), 1, PAGE)
    length_rows = (page_count - 1) * PAGE + spread
    at_most = (local_rank == 0) | long_one & (local_rank == N_REQ)
    length_rows = jnp.where(at_most, page_count * PAGE - 1, length_rows)
    offsets = jnp.cumsum(page_count, axis=1) - page_count
    shuffle = permute_rows(jax.random.fold_in(key, 15), N_REQ, POOL_DEV)
    slot_ids = jnp.arange(MAXP, dtype=jnp.int32)
    table_pos = offsets[:, :, None] + jnp.minimum(slot_ids[None, None, :], page_count[:, :, None] - 1)
    page_rows = jnp.take_along_axis(shuffle, table_pos.reshape(N_REQ, R_DEV * MAXP), axis=1)
    page_rows = page_rows.reshape(N_REQ * R_DEV, MAXP)
    mig_rows = jnp.argsort(local_rank, axis=1)[:, :N_REQ]
    return (length_rows.reshape(N_REQ * R_DEV).astype(jnp.int32), page_rows.astype(jnp.int32), mig_rows.astype(jnp.int32))


def draw_lengths(key, part):
    return layout(key)[0]


def draw_page_table(key, part):
    return layout(key)[1]


def draw_mig_request(key, part):
    return layout(key)[2]


def draw_mig_dest(key, part):
    return permute_rows(jax.random.fold_in(key, 16), N_REQ, N_REQ).astype(jnp.int32)


def draw_k_pool(key, part):
    full_shape = (N_REQ * POOL_DEV, PAGE, KVH * HD)
    base_draw = jnp.clip(jax.random.normal(jax.random.fold_in(key, 21), full_shape, jnp.float32), -3.0, 3.0)
    return base_draw.astype(jnp.bfloat16)


def block_levels(stream_key, dims, cuts, low, largest):
    gain = 1.0
    for dim, parts in cuts:
        draws = jax.random.uniform(jax.random.fold_in(jax.random.fold_in(stream_key, 6), dim), (parts,), jnp.float32, low / len(cuts), largest / len(cuts))
        gain = gain * jnp.repeat(jnp.exp(draws), dims[dim] // parts).reshape((-1,) + (1,) * (len(dims) - 1 - dim))
    return gain


def bell_draw(stream_key, dims, deviation, most, cuts=(), kind=jnp.bfloat16):
    entries = deviation * jax.random.normal(stream_key, dims, jnp.float32)
    if cuts:
        entries = entries * block_levels(stream_key, dims, cuts, -0.22, 0.18)
    return jnp.clip(entries, -most, most).astype(kind)


def setup_inputs(seed: int = 0) -> dict:
    key_of = jax.random.split(jax.random.key(seed), 20)
    return {
        "hidden": bell_draw(key_of[0], (REQS, D), 1.0, 6.0, ((0, 16), (1, 8))),
        "attn_gain": jnp.clip(1.0 + 0.15 * jax.random.normal(key_of[1], (D,), jnp.float32), 0.25, 1.75),
        "q_gain": jnp.clip(1.0 + 0.15 * jax.random.normal(key_of[2], (HD,), jnp.float32), 0.25, 1.75),
        "k_gain": jnp.clip(1.0 + 0.15 * jax.random.normal(key_of[3], (HD,), jnp.float32), 0.25, 1.75),
        "w_q": bell_draw(key_of[4], (D, H * HD), D ** -0.5, 0.125, ((1, 8),)),
        "w_gate_attn": bell_draw(key_of[5], (D, H * HD), D ** -0.5, 0.125, ((1, 8),)),
        "w_k": bell_draw(key_of[6], (D, KVH * HD), D ** -0.5, 0.125, ((1, 8),)),
        "w_v": bell_draw(key_of[7], (D, KVH * HD), D ** -0.5, 0.125, ((1, 8),)),
        "w_o": bell_draw(key_of[8], (H * HD, D), (H * HD) ** -0.5, 0.125, ((0, 8),)),
        "k_pool": draw_k_pool(jax.random.fold_in(key_of[19], 71), 0),
        "v_pool": bell_draw(key_of[10], (N_REQ * POOL_DEV, PAGE, KVH * HD), 1.0, 6.0, ((0, 16), (2, 8))),
        "lengths": draw_lengths(jax.random.fold_in(key_of[19], 71), 0),
        "page_table": draw_page_table(jax.random.fold_in(key_of[19], 71), 0),
        "mig_request": draw_mig_request(jax.random.fold_in(key_of[19], 71), 0),
        "mig_dest": draw_mig_dest(jax.random.fold_in(key_of[19], 71), 0),
        "mlp_gain": jnp.clip(1.0 + 0.15 * jax.random.normal(key_of[15], (D,), jnp.float32), 0.25, 1.75),
        "w_gate": bell_draw(key_of[16], (D, FF), D ** -0.5, 0.125, ((1, 128),)),
        "w_up": bell_draw(key_of[17], (D, FF), D ** -0.5, 0.125, ((1, 128),)),
        "w_down": bell_draw(key_of[18], (D, FF), FF ** -0.5, 0.078125, ((1, 128),)),
    }


EPSILON = 1e-06
ROPE_BASE = 1000000.0

def rms_norm(values, scale_row):
    values = values.astype(jnp.float32)
    return values * lax.rsqrt(lax.optimization_barrier(jnp.mean(values * values, axis=-1, keepdims=True)) + EPSILON) * scale_row

def rotate(values, position):
    half_dim = values.shape[-1] // 2
    frequency = ROPE_BASE ** (-jnp.arange(half_dim, dtype=jnp.float32) * 2.0 / values.shape[-1])
    angles = position.astype(jnp.float32)[:, None, None] * frequency
    cosine = jnp.cos(angles)
    sine_part = jnp.sin(angles)
    first_half = values[..., :half_dim]
    second = values[..., half_dim:]
    return jnp.concatenate([first_half * cosine - second * sine_part, second * cosine + first_half * sine_part], axis=-1)

def reference(hidden, attn_gain, q_gain, k_gain, w_q, w_gate_attn, w_k, w_v, w_o, k_pool, v_pool, lengths, page_table, mig_request, mig_dest, mlp_gain, w_gate, w_up, w_down):
    group_size = H // KVH
    slot_span = MAXP * PAGE
    score_scale = HD ** (-0.5)
    normed = rms_norm(hidden, attn_gain).astype(jnp.bfloat16)
    query_raw = jnp.dot(normed, w_q, preferred_element_type=jnp.float32).reshape(REQS, H, HD)
    gate_raw = jnp.dot(normed, w_gate_attn, preferred_element_type=jnp.float32)
    key_raw = jnp.dot(normed, w_k, preferred_element_type=jnp.float32).reshape(REQS, KVH, HD)
    value_raw = jnp.dot(normed, w_v, preferred_element_type=jnp.float32).reshape(REQS, KVH, HD)
    queries = rotate(rms_norm(query_raw, q_gain), lengths).astype(jnp.bfloat16)
    new_keys = rotate(rms_norm(key_raw, k_gain), lengths).astype(jnp.bfloat16)
    new_values = value_raw.astype(jnp.bfloat16)
    owners = jnp.arange(REQS, dtype=jnp.int32) // R_DEV
    pool_pages = page_table + (owners * POOL_DEV)[:, None]
    position = jnp.arange(slot_span, dtype=jnp.int32)

    def attend(request_items):
        one_query, key_new, value_new, page_ids, length = request_items
        cached_keys = k_pool[page_ids].reshape(slot_span, KVH, HD).astype(jnp.float32)
        cached_values = v_pool[page_ids].reshape(slot_span, KVH, HD).astype(jnp.float32)
        grouped = one_query.astype(jnp.float32).reshape(KVH, group_size, HD)
        scores = jnp.einsum('kgd,tkd->kgt', grouped, cached_keys) * score_scale
        scores = jnp.where(position < length, scores, -jnp.inf)
        own_score = jnp.einsum('kgd,kd->kg', grouped, key_new.astype(jnp.float32)) * score_scale
        row_top = jnp.maximum(lax.optimization_barrier(jnp.max(scores, axis=-1)), own_score)
        exps_all = jnp.exp(scores - row_top[..., None])
        own_exp = jnp.exp(own_score - row_top)
        denom_sum = lax.optimization_barrier(jnp.sum(exps_all, axis=-1)) + own_exp
        weights = lax.optimization_barrier((exps_all / denom_sum[..., None]).astype(jnp.bfloat16)).astype(jnp.float32)
        own_weight = lax.optimization_barrier((own_exp / denom_sum).astype(jnp.bfloat16)).astype(jnp.float32)
        context = jnp.einsum('kgt,tkd->kgd', weights, cached_values)
        context = context + own_weight[..., None] * value_new.astype(jnp.float32)[:, None, :]
        return context.reshape(H * HD)
    context = lax.map(attend, (queries, new_keys, new_values, pool_pages, lengths))
    gated = (jax.nn.sigmoid(gate_raw) * context).astype(jnp.bfloat16)
    mid_stream = (hidden.astype(jnp.float32) + jnp.dot(gated, w_o, preferred_element_type=jnp.float32)).astype(jnp.bfloat16)
    normed_mlp = rms_norm(mid_stream, mlp_gain).astype(jnp.bfloat16)
    gate_part = jnp.dot(normed_mlp, w_gate, preferred_element_type=jnp.float32)
    up_part = jnp.dot(normed_mlp, w_up, preferred_element_type=jnp.float32)
    activation = (jax.nn.silu(gate_part) * up_part).astype(jnp.bfloat16)
    down_part = jnp.dot(activation, w_down.T, preferred_element_type=jnp.float32)
    out_hidden = (mid_stream.astype(jnp.float32) + down_part).astype(jnp.bfloat16)
    src_flat = jnp.repeat(jnp.arange(N_REQ, dtype=jnp.int32), N_REQ)
    moved_rows = src_flat * R_DEV + mig_request.reshape(-1).astype(jnp.int32)
    moved_pages = page_table[moved_rows, :MIGP] + (src_flat * POOL_DEV)[:, None]
    slot_count = MIGP * PAGE
    slot_pos = jnp.arange(slot_count, dtype=jnp.int32)[None, :, None]
    moved_len = lengths[moved_rows][:, None, None]
    zero_value = jnp.zeros((), jnp.bfloat16)
    target = mig_dest.reshape(-1).astype(jnp.int32) * N_REQ + src_flat

    def place_cache(pool, fresh_rows):
        cached = pool[moved_pages].reshape(N_REQ * N_REQ, slot_count, KVH * HD)
        fresh_row = fresh_rows.reshape(REQS, KVH * HD)[moved_rows][:, None, :]
        filled = jnp.where(slot_pos < moved_len, cached, jnp.where(slot_pos == moved_len, fresh_row, zero_value))
        return jnp.zeros((N_REQ * N_REQ, slot_count, KVH * HD), jnp.bfloat16).at[target].set(filled)
    mig_keys = place_cache(k_pool, new_keys)
    mig_values = place_cache(v_pool, new_values)
    return (out_hidden, mig_keys, mig_values)
```

```python
import jax
import jax.numpy as jnp
from jax import lax
from jax.sharding import PartitionSpec as P

MIGP = 4


EPSILON = 1e-06
ROPE_BASE = 1000000.0
SLOT_BLOCK = 4


def rms_norm(values, scale_row):
    values = values.astype(jnp.float32)
    return (
        values * lax.rsqrt(jnp.mean(values * values, axis=-1, keepdims=True) + EPSILON) * scale_row
    )


def rotate(values, position):
    half_dim = values.shape[-1] // 2
    frequency = ROPE_BASE ** (-jnp.arange(half_dim, dtype=jnp.float32) * 2.0 / values.shape[-1])
    angles = position.astype(jnp.float32)[:, None, None] * frequency
    cosine = jnp.cos(angles)
    sine_part = jnp.sin(angles)
    first_half = values[..., :half_dim]
    second = values[..., half_dim:]
    return jnp.concatenate(
        [first_half * cosine - second * sine_part, second * cosine + first_half * sine_part],
        axis=-1,
    )


def attend_slots(queries, new_keys, new_values, k_pool, v_pool, lengths, page_table):
    req_count, kv_local, group_size, head_dim = queries.shape
    page_size = k_pool.shape[1]
    slot_span = page_table.shape[1] * page_size
    score_scale = head_dim ** (-0.5)
    used_pages = jnp.max(lengths) // page_size + 1
    turn_count = (used_pages + SLOT_BLOCK - 1) // SLOT_BLOCK
    block_width = SLOT_BLOCK * page_size

    def score_block(turn_index, buffer):
        page_ids = lax.dynamic_slice_in_dim(page_table, turn_index * SLOT_BLOCK, SLOT_BLOCK, 1)
        key_block = k_pool[page_ids].reshape(req_count, block_width, kv_local, head_dim)
        scores = (
            jnp.einsum("rkgd,rtkd->rkgt", queries, key_block, preferred_element_type=jnp.float32)
            * score_scale
        )
        return lax.dynamic_update_slice_in_dim(buffer, scores, turn_index * block_width, 3)

    start_buffer = jnp.full((req_count, kv_local, group_size, slot_span), -jnp.inf, jnp.float32)
    scores = lax.fori_loop(0, turn_count, score_block, start_buffer)
    position = jnp.arange(slot_span, dtype=jnp.int32)
    scores = jnp.where(
        position[None, None, None, :] < lengths[:, None, None, None], scores, -jnp.inf
    )
    own_score = (
        jnp.einsum("rkgd,rkd->rkg", queries, new_keys, preferred_element_type=jnp.float32)
        * score_scale
    )
    row_top = jnp.maximum(jnp.max(scores, axis=-1), own_score)
    exps_all = jnp.exp(scores - row_top[..., None])
    own_exp = jnp.exp(own_score - row_top)
    denom_sum = jnp.sum(exps_all, axis=-1) + own_exp
    weights = (exps_all / denom_sum[..., None]).astype(jnp.bfloat16)
    own_weight = (own_exp / denom_sum).astype(jnp.bfloat16)

    def value_block(turn_index, context_sum):
        page_ids = lax.dynamic_slice_in_dim(page_table, turn_index * SLOT_BLOCK, SLOT_BLOCK, 1)
        val_block = v_pool[page_ids].reshape(req_count, block_width, kv_local, head_dim)
        weight_block = lax.dynamic_slice_in_dim(weights, turn_index * block_width, block_width, 3)
        return context_sum + jnp.einsum(
            "rkgt,rtkd->rkgd", weight_block, val_block, preferred_element_type=jnp.float32
        )

    start_sum = jnp.einsum(
        "rkg,rkd->rkgd", own_weight, new_values, preferred_element_type=jnp.float32
    )
    return lax.fori_loop(0, turn_count, value_block, start_sum)


def reduce_to_slice(partial, kv_count, slice_width):
    rows = partial.shape[0]
    pieces = partial.reshape(rows, kv_count, slice_width).transpose(1, 0, 2)
    arrived = lax.all_to_all(pieces, "kv", 0, 0, tiled=True)
    return jnp.sum(arrived, axis=0)


def per_device(
    hidden,
    attn_gain,
    q_gain,
    k_gain,
    w_q,
    w_gate_attn,
    w_k,
    w_v,
    w_o,
    k_pool,
    v_pool,
    lengths,
    page_table,
    mig_request,
    mig_dest,
    mlp_gain,
    w_gate,
    w_up,
    w_down,
):
    head_dim = q_gain.shape[0]
    req_count = hidden.shape[0]
    kv_local = w_k.shape[1] // head_dim
    q_local = w_q.shape[1] // head_dim
    group_size = q_local // kv_local
    page_size = k_pool.shape[1]
    channels = kv_local * head_dim
    model_width = mlp_gain.shape[0]
    gate_w = lax.all_gather(w_gate, "req", axis=1, tiled=True)
    up_w = lax.all_gather(w_up, "req", axis=1, tiled=True)
    down_w = lax.all_gather(w_down, "req", axis=1, tiled=True)
    whole_rows = lax.all_gather(hidden, "kv", axis=1, tiled=True)
    normed = rms_norm(whole_rows, attn_gain).astype(jnp.bfloat16)
    query_raw = jnp.dot(normed, w_q, preferred_element_type=jnp.float32).reshape(
        req_count, q_local, head_dim
    )
    gate_raw = jnp.dot(normed, w_gate_attn, preferred_element_type=jnp.float32)
    key_raw = jnp.dot(normed, w_k, preferred_element_type=jnp.float32).reshape(
        req_count, kv_local, head_dim
    )
    value_raw = jnp.dot(normed, w_v, preferred_element_type=jnp.float32).reshape(
        req_count, kv_local, head_dim
    )
    queries = rotate(rms_norm(query_raw, q_gain), lengths).astype(jnp.bfloat16)
    queries = queries.reshape(req_count, kv_local, group_size, head_dim)
    new_keys = rotate(rms_norm(key_raw, k_gain), lengths).astype(jnp.bfloat16)
    new_values = value_raw.astype(jnp.bfloat16)
    mig_rows = mig_request[0]
    dest_row = mig_dest[0]
    mig_count = mig_rows.shape[0]
    slot_count = MIGP * page_size
    moved_pages = page_table[mig_rows, :MIGP]
    slot_pos = jnp.arange(slot_count, dtype=jnp.int32)[None, :, None]
    moved_len = lengths[mig_rows][:, None, None]
    zero_value = jnp.zeros((), jnp.bfloat16)
    inverse = jnp.zeros_like(dest_row).at[dest_row].set(jnp.arange(mig_count, dtype=jnp.int32))

    def place_cache(pool, fresh_rows):
        cached = pool[moved_pages].reshape(mig_count, slot_count, channels)
        fresh_row = fresh_rows.reshape(req_count, channels)[mig_rows][:, None, :]
        filled = jnp.where(
            slot_pos < moved_len, cached, jnp.where(slot_pos == moved_len, fresh_row, zero_value)
        )
        return filled[inverse]

    mig_keys, mig_values = (
        lax.all_to_all(
            place_cache(k_pool, new_keys), "req", split_axis=0, concat_axis=0, tiled=True
        ),
        lax.all_to_all(
            place_cache(v_pool, new_values), "req", split_axis=0, concat_axis=0, tiled=True
        ),
    )
    context = attend_slots(queries, new_keys, new_values, k_pool, v_pool, lengths, page_table)
    gated = (jax.nn.sigmoid(gate_raw) * context.reshape(req_count, q_local * head_dim)).astype(
        jnp.bfloat16
    )
    head_terms = jnp.dot(gated, w_o, preferred_element_type=jnp.float32)
    kv_count = lax.axis_size("kv")
    slice_width = model_width // kv_count
    mid_slice = (
        hidden.astype(jnp.float32) + reduce_to_slice(head_terms, kv_count, slice_width)
    ).astype(jnp.bfloat16)
    mid_stream = lax.all_gather(mid_slice, "kv", axis=1, tiled=True)
    normed_mlp = rms_norm(mid_stream, mlp_gain).astype(jnp.bfloat16)
    gate_part = jnp.dot(normed_mlp, gate_w, preferred_element_type=jnp.float32)
    up_part = jnp.dot(normed_mlp, up_w, preferred_element_type=jnp.float32)
    activation = (jax.nn.silu(gate_part) * up_part).astype(jnp.bfloat16)
    down_part = jnp.einsum(
        "ru,cu->rc", activation, down_w, preferred_element_type=jnp.float32
    )
    mlp_part = reduce_to_slice(down_part, kv_count, slice_width)
    out_hidden = (mid_slice.astype(jnp.float32) + mlp_part).astype(jnp.bfloat16)
    return (out_hidden, mig_keys, mig_values)


def solution(mesh):
    return jax.shard_map(
        per_device,
        mesh=mesh,
        in_specs=(
            P("req", "kv"),
            P(),
            P(),
            P(),
            P(None, "kv"),
            P(None, "kv"),
            P(None, "kv"),
            P(None, "kv"),
            P("kv", None),
            P("req", None, "kv"),
            P("req", None, "kv"),
            P("req"),
            P("req", None),
            P("req", None),
            P("req", None),
            P(),
            P(None, ("req", "kv")),
            P(None, ("req", "kv")),
            P(None, ("req", "kv")),
        ),
        out_specs=(P("req", "kv"), P("req", None, "kv"), P("req", None, "kv")),
        check_vma=False,
    )
```

```python
import jax
import jax.numpy as jnp
from jax import lax
from jax.sharding import PartitionSpec as P

MIGP = 4


EPSILON = 1e-06
ROPE_BASE = 1000000.0


def rms_norm(values, scale_row):
    values = values.astype(jnp.float32)
    return (
        values * lax.rsqrt(jnp.mean(values * values, axis=-1, keepdims=True) + EPSILON) * scale_row
    )


def rotate(values, position):
    half_dim = values.shape[-1] // 2
    frequency = ROPE_BASE ** (-jnp.arange(half_dim, dtype=jnp.float32) * 2.0 / values.shape[-1])
    angles = position.astype(jnp.float32)[:, None, None] * frequency
    cosine = jnp.cos(angles)
    sine_part = jnp.sin(angles)
    first_half = values[..., :half_dim]
    second = values[..., half_dim:]
    return jnp.concatenate(
        [first_half * cosine - second * sine_part, second * cosine + first_half * sine_part],
        axis=-1,
    )


def attend_pool(queries, new_keys, new_values, k_pool, v_pool, lengths, page_table):
    req_count, kv_local, group_size, head_dim = queries.shape
    pool_pages, page_size, _ = k_pool.shape
    table_width = page_table.shape[1]
    token_count = pool_pages * page_size
    score_scale = head_dim ** (-0.5)
    slot_ids = jnp.arange(table_width, dtype=jnp.int32)
    in_use = slot_ids[None, :] < (lengths // page_size + 1)[:, None]
    targets = jnp.where(in_use, page_table, pool_pages).reshape(-1)
    owner = (
        jnp.full((pool_pages,), -1, jnp.int32)
        .at[targets]
        .set(jnp.repeat(jnp.arange(req_count, dtype=jnp.int32), table_width), mode="drop")
    )
    first_pos = (
        jnp.zeros((pool_pages,), jnp.int32)
        .at[targets]
        .set(jnp.tile(slot_ids * page_size, req_count), mode="drop")
    )
    token_owner = jnp.repeat(owner, page_size)
    token_pos = (first_pos[:, None] + jnp.arange(page_size, dtype=jnp.int32)[None, :]).reshape(-1)
    valid = (token_owner[None, :] == jnp.arange(req_count, dtype=jnp.int32)[:, None]) & (
        token_pos[None, :] < lengths[:, None]
    )
    keys = k_pool.reshape(token_count, kv_local, head_dim)
    values = v_pool.reshape(token_count, kv_local, head_dim)
    scores = (
        jnp.einsum("rkgd,tkd->rkgt", queries, keys, preferred_element_type=jnp.float32)
        * score_scale
    )
    scores = jnp.where(valid[:, None, None, :], scores, -jnp.inf)
    own_score = (
        jnp.einsum("rkgd,rkd->rkg", queries, new_keys, preferred_element_type=jnp.float32)
        * score_scale
    )
    row_top = jnp.maximum(jnp.max(scores, axis=-1), own_score)
    exps_all = jnp.exp(scores - row_top[..., None])
    own_exp = jnp.exp(own_score - row_top)
    denom_sum = jnp.sum(exps_all, axis=-1) + own_exp
    weights = (exps_all / denom_sum[..., None]).astype(jnp.bfloat16)
    own_weight = (own_exp / denom_sum).astype(jnp.bfloat16)
    start_sum = jnp.einsum(
        "rkg,rkd->rkgd", own_weight, new_values, preferred_element_type=jnp.float32
    )
    return start_sum + jnp.einsum(
        "rkgt,tkd->rkgd", weights, values, preferred_element_type=jnp.float32
    )


def reduce_to_slice(partial, kv_count, slice_width):
    rows = partial.shape[0]
    pieces = partial.reshape(rows, kv_count, slice_width).transpose(1, 0, 2)
    arrived = lax.all_to_all(pieces, "kv", 0, 0, tiled=True)
    return jnp.sum(arrived, axis=0)


def per_device(
    hidden,
    attn_gain,
    q_gain,
    k_gain,
    w_q,
    w_gate_attn,
    w_k,
    w_v,
    w_o,
    k_pool,
    v_pool,
    lengths,
    page_table,
    mig_request,
    mig_dest,
    mlp_gain,
    w_gate,
    w_up,
    w_down,
):
    head_dim = q_gain.shape[0]
    req_count = hidden.shape[0]
    kv_local = w_k.shape[1] // head_dim
    q_local = w_q.shape[1] // head_dim
    group_size = q_local // kv_local
    page_size = k_pool.shape[1]
    channels = kv_local * head_dim
    model_width = mlp_gain.shape[0]
    gate_w = lax.all_gather(w_gate, "req", axis=1, tiled=True)
    up_w = lax.all_gather(w_up, "req", axis=1, tiled=True)
    down_w = lax.all_gather(w_down, "req", axis=1, tiled=True)
    whole_rows = lax.all_gather(hidden, "kv", axis=1, tiled=True)
    normed = rms_norm(whole_rows, attn_gain).astype(jnp.bfloat16)
    query_raw = jnp.dot(normed, w_q, preferred_element_type=jnp.float32).reshape(
        req_count, q_local, head_dim
    )
    gate_raw = jnp.dot(normed, w_gate_attn, preferred_element_type=jnp.float32)
    key_raw = jnp.dot(normed, w_k, preferred_element_type=jnp.float32).reshape(
        req_count, kv_local, head_dim
    )
    value_raw = jnp.dot(normed, w_v, preferred_element_type=jnp.float32).reshape(
        req_count, kv_local, head_dim
    )
    queries = rotate(rms_norm(query_raw, q_gain), lengths).astype(jnp.bfloat16)
    queries = queries.reshape(req_count, kv_local, group_size, head_dim)
    new_keys = rotate(rms_norm(key_raw, k_gain), lengths).astype(jnp.bfloat16)
    new_values = value_raw.astype(jnp.bfloat16)
    mig_rows = mig_request[0]
    dest_row = mig_dest[0]
    mig_count = mig_rows.shape[0]
    slot_count = MIGP * page_size
    moved_pages = page_table[mig_rows, :MIGP]
    slot_pos = jnp.arange(slot_count, dtype=jnp.int32)[None, :, None]
    moved_len = lengths[mig_rows][:, None, None]
    zero_value = jnp.zeros((), jnp.bfloat16)
    inverse = jnp.zeros_like(dest_row).at[dest_row].set(jnp.arange(mig_count, dtype=jnp.int32))

    def place_cache(pool, fresh_rows):
        cached = pool[moved_pages].reshape(mig_count, slot_count, channels)
        fresh_row = fresh_rows.reshape(req_count, channels)[mig_rows][:, None, :]
        filled = jnp.where(
            slot_pos < moved_len, cached, jnp.where(slot_pos == moved_len, fresh_row, zero_value)
        )
        return filled[inverse]

    mig_keys, mig_values = (
        lax.all_to_all(
            place_cache(k_pool, new_keys), "req", split_axis=0, concat_axis=0, tiled=True
        ),
        lax.all_to_all(
            place_cache(v_pool, new_values), "req", split_axis=0, concat_axis=0, tiled=True
        ),
    )
    context = attend_pool(queries, new_keys, new_values, k_pool, v_pool, lengths, page_table)
    gated = (jax.nn.sigmoid(gate_raw) * context.reshape(req_count, q_local * head_dim)).astype(
        jnp.bfloat16
    )
    head_terms = jnp.dot(gated, w_o, preferred_element_type=jnp.float32)
    kv_count = lax.axis_size("kv")
    slice_width = model_width // kv_count
    mid_slice = (
        hidden.astype(jnp.float32) + reduce_to_slice(head_terms, kv_count, slice_width)
    ).astype(jnp.bfloat16)
    mid_stream = lax.all_gather(mid_slice, "kv", axis=1, tiled=True)
    normed_mlp = rms_norm(mid_stream, mlp_gain).astype(jnp.bfloat16)
    gate_part = jnp.dot(normed_mlp, gate_w, preferred_element_type=jnp.float32)
    up_part = jnp.dot(normed_mlp, up_w, preferred_element_type=jnp.float32)
    activation = (jax.nn.silu(gate_part) * up_part).astype(jnp.bfloat16)
    down_part = jnp.einsum(
        "ru,cu->rc", activation, down_w, preferred_element_type=jnp.float32
    )
    mlp_part = reduce_to_slice(down_part, kv_count, slice_width)
    out_hidden = (mid_slice.astype(jnp.float32) + mlp_part).astype(jnp.bfloat16)
    return (out_hidden, mig_keys, mig_values)


def solution(mesh):
    return jax.shard_map(
        per_device,
        mesh=mesh,
        in_specs=(
            P("req", "kv"),
            P(),
            P(),
            P(),
            P(None, "kv"),
            P(None, "kv"),
            P(None, "kv"),
            P(None, "kv"),
            P("kv", None),
            P("req", None, "kv"),
            P("req", None, "kv"),
            P("req"),
            P("req", None),
            P("req", None),
            P("req", None),
            P(),
            P(None, ("req", "kv")),
            P(None, ("req", "kv")),
            P(None, ("req", "kv")),
        ),
        out_specs=(P("req", "kv"), P("req", None, "kv"), P("req", None, "kv")),
        check_vma=False,
    )
```

```python
import jax
import jax.numpy as jnp
from jax import lax
from jax.sharding import PartitionSpec as P

MIGP = 4


EPSILON = 1e-06
ROPE_BASE = 1000000.0


def rms_norm(values, scale_row):
    values = values.astype(jnp.float32)
    return (
        values * lax.rsqrt(jnp.mean(values * values, axis=-1, keepdims=True) + EPSILON) * scale_row
    )


def rotate(values, position):
    half_dim = values.shape[-1] // 2
    frequency = ROPE_BASE ** (-jnp.arange(half_dim, dtype=jnp.float32) * 2.0 / values.shape[-1])
    angles = position.astype(jnp.float32)[:, None, None] * frequency
    cosine = jnp.cos(angles)
    sine_part = jnp.sin(angles)
    first_half = values[..., :half_dim]
    second = values[..., half_dim:]
    return jnp.concatenate(
        [first_half * cosine - second * sine_part, second * cosine + first_half * sine_part],
        axis=-1,
    )


def attend_pool(queries, new_keys, new_values, k_pool, v_pool, lengths, page_table):
    req_count, kv_local, _, head_dim = queries.shape
    pool_pages, page_size, _ = k_pool.shape
    table_width = page_table.shape[1]
    token_count = pool_pages * page_size
    score_scale = head_dim ** (-0.5)
    slot_ids = jnp.arange(table_width, dtype=jnp.int32)
    in_use = slot_ids[None, :] < (lengths // page_size + 1)[:, None]
    match = (
        page_table[:, :, None] == jnp.arange(pool_pages, dtype=jnp.int32)[None, None, :]
    ) & in_use[:, :, None]
    page_mine = jnp.any(match, axis=1)
    page_start = jnp.sum(jnp.where(match, slot_ids[None, :, None] * page_size, 0), axis=1)
    token_pos = page_start[:, :, None] + jnp.arange(page_size, dtype=jnp.int32)[None, None, :]
    valid = (page_mine[:, :, None] & (token_pos < lengths[:, None, None])).reshape(
        req_count, token_count
    )
    keys = k_pool.reshape(token_count, kv_local, head_dim)
    values = v_pool.reshape(token_count, kv_local, head_dim)
    scores = (
        jnp.einsum("rkgd,tkd->rkgt", queries, keys, preferred_element_type=jnp.float32)
        * score_scale
    )
    scores = jnp.where(valid[:, None, None, :], scores, -jnp.inf)
    own_score = (
        jnp.einsum("rkgd,rkd->rkg", queries, new_keys, preferred_element_type=jnp.float32)
        * score_scale
    )
    row_top = jnp.maximum(jnp.max(scores, axis=-1), own_score)
    exps_all = jnp.exp(scores - row_top[..., None])
    own_exp = jnp.exp(own_score - row_top)
    denom_sum = jnp.sum(exps_all, axis=-1) + own_exp
    weights = (exps_all / denom_sum[..., None]).astype(jnp.bfloat16)
    own_weight = (own_exp / denom_sum).astype(jnp.bfloat16)
    start_sum = jnp.einsum(
        "rkg,rkd->rkgd", own_weight, new_values, preferred_element_type=jnp.float32
    )
    return start_sum + jnp.einsum(
        "rkgt,tkd->rkgd", weights, values, preferred_element_type=jnp.float32
    )


def reduce_to_slice(partial, kv_count, slice_width):
    rows = partial.shape[0]
    pieces = partial.reshape(rows, kv_count, slice_width).transpose(1, 0, 2)
    arrived = lax.all_to_all(pieces, "kv", 0, 0, tiled=True)
    return jnp.sum(arrived, axis=0)


def layer_body(
    hidden,
    attn_gain,
    q_gain,
    k_gain,
    w_q,
    w_gate_attn,
    w_k,
    w_v,
    w_o,
    k_pool,
    v_pool,
    lengths,
    page_table,
    mig_request,
    mig_dest,
    mlp_gain,
    w_gate,
    w_up,
    w_down,
):
    head_dim = q_gain.shape[0]
    req_count = hidden.shape[0]
    kv_local = w_k.shape[1] // head_dim
    q_local = w_q.shape[1] // head_dim
    group_size = q_local // kv_local
    page_size = k_pool.shape[1]
    channels = kv_local * head_dim
    model_width = mlp_gain.shape[0]
    unit_count = w_gate.shape[1]
    stacked = lax.all_gather(
        jnp.concatenate([w_gate, w_up, w_down], axis=1), "req", axis=0, tiled=False
    )
    gate_w = stacked[:, :, :unit_count]
    up_w = stacked[:, :, unit_count : 2 * unit_count]
    down_w = stacked[:, :, 2 * unit_count :]
    whole_rows = lax.all_gather(hidden, "kv", axis=1, tiled=True)
    normed = rms_norm(whole_rows, attn_gain).astype(jnp.bfloat16)
    query_raw = jnp.dot(normed, w_q, preferred_element_type=jnp.float32).reshape(
        req_count, q_local, head_dim
    )
    gate_raw = jnp.dot(normed, w_gate_attn, preferred_element_type=jnp.float32)
    key_raw = jnp.dot(normed, w_k, preferred_element_type=jnp.float32).reshape(
        req_count, kv_local, head_dim
    )
    value_raw = jnp.dot(normed, w_v, preferred_element_type=jnp.float32).reshape(
        req_count, kv_local, head_dim
    )
    queries = rotate(rms_norm(query_raw, q_gain), lengths).astype(jnp.bfloat16)
    queries = queries.reshape(req_count, kv_local, group_size, head_dim)
    new_keys = rotate(rms_norm(key_raw, k_gain), lengths).astype(jnp.bfloat16)
    new_values = value_raw.astype(jnp.bfloat16)
    mig_rows = mig_request[0]
    dest_row = mig_dest[0]
    mig_count = mig_rows.shape[0]
    slot_count = MIGP * page_size
    moved_pages = page_table[mig_rows, :MIGP]
    slot_pos = jnp.arange(slot_count, dtype=jnp.int32)[None, :, None]
    moved_len = lengths[mig_rows][:, None, None]
    zero_value = jnp.zeros((), jnp.bfloat16)
    inverse = jnp.zeros_like(dest_row).at[dest_row].set(jnp.arange(mig_count, dtype=jnp.int32))

    def place_cache(pool, fresh_rows):
        cached = pool[moved_pages].reshape(mig_count, slot_count, channels)
        fresh_row = fresh_rows.reshape(req_count, channels)[mig_rows][:, None, :]
        filled = jnp.where(
            slot_pos < moved_len, cached, jnp.where(slot_pos == moved_len, fresh_row, zero_value)
        )
        return filled[inverse]

    mig_keys, mig_values = (
        lax.all_to_all(
            place_cache(k_pool, new_keys), "req", split_axis=0, concat_axis=0, tiled=True
        ),
        lax.all_to_all(
            place_cache(v_pool, new_values), "req", split_axis=0, concat_axis=0, tiled=True
        ),
    )
    context = attend_pool(queries, new_keys, new_values, k_pool, v_pool, lengths, page_table)
    gated = (jax.nn.sigmoid(gate_raw) * context.reshape(req_count, q_local * head_dim)).astype(
        jnp.bfloat16
    )
    head_terms = jnp.dot(gated, w_o, preferred_element_type=jnp.float32)
    kv_count = lax.axis_size("kv")
    slice_width = model_width // kv_count
    mid_slice = (
        hidden.astype(jnp.float32) + reduce_to_slice(head_terms, kv_count, slice_width)
    ).astype(jnp.bfloat16)
    mid_stream = lax.all_gather(mid_slice, "kv", axis=1, tiled=True)
    normed_mlp = rms_norm(mid_stream, mlp_gain).astype(jnp.bfloat16)
    gate_part = jnp.einsum("rd,sdu->rsu", normed_mlp, gate_w, preferred_element_type=jnp.float32)
    up_part = jnp.einsum("rd,sdu->rsu", normed_mlp, up_w, preferred_element_type=jnp.float32)
    activation = (jax.nn.silu(gate_part) * up_part).astype(jnp.bfloat16)
    down_part = jnp.einsum(
        "rsu,scu->rc", activation, down_w, preferred_element_type=jnp.float32
    )
    mlp_part = reduce_to_slice(down_part, kv_count, slice_width)
    out_hidden = (mid_slice.astype(jnp.float32) + mlp_part).astype(jnp.bfloat16)
    return (out_hidden, mig_keys, mig_values)


def solution(mesh):
    return jax.shard_map(
        layer_body,
        mesh=mesh,
        in_specs=(
            P("req", "kv"),
            P(),
            P(),
            P(),
            P(None, "kv"),
            P(None, "kv"),
            P(None, "kv"),
            P(None, "kv"),
            P("kv", None),
            P("req", None, "kv"),
            P("req", None, "kv"),
            P("req"),
            P("req", None),
            P("req", None),
            P("req", None),
            P(),
            P(None, ("req", "kv")),
            P(None, ("req", "kv")),
            P(None, ("req", "kv")),
        ),
        out_specs=(P("req", "kv"), P("req", None, "kv"), P("req", None, "kv")),
        check_vma=False,
    )
```

```python
import jax
import jax.numpy as jnp
from jax import lax
from jax.sharding import PartitionSpec as P

MIGP = 4


EPSILON = 1e-06
ROPE_BASE = 1000000.0


def rms_norm(values, scale_row):
    values = values.astype(jnp.float32)
    return (
        values * lax.rsqrt(jnp.mean(values * values, axis=-1, keepdims=True) + EPSILON) * scale_row
    )


def rotate(values, position):
    half_dim = values.shape[-1] // 2
    frequency = ROPE_BASE ** (-jnp.arange(half_dim, dtype=jnp.float32) * 2.0 / values.shape[-1])
    angles = position.astype(jnp.float32)[:, None, None] * frequency
    cosine = jnp.cos(angles)
    sine_part = jnp.sin(angles)
    first_half = values[..., :half_dim]
    second = values[..., half_dim:]
    return jnp.concatenate(
        [first_half * cosine - second * sine_part, second * cosine + first_half * sine_part],
        axis=-1,
    )


def attend_pool(queries, new_keys, new_values, k_pool, v_pool, lengths, page_table):
    req_count, kv_local, _, head_dim = queries.shape
    pool_pages, page_size, _ = k_pool.shape
    table_width = page_table.shape[1]
    token_count = pool_pages * page_size
    score_scale = head_dim ** (-0.5)
    slot_ids = jnp.arange(table_width, dtype=jnp.int32)
    in_use = slot_ids[None, :] < (lengths // page_size + 1)[:, None]
    match = (
        page_table[:, :, None] == jnp.arange(pool_pages, dtype=jnp.int32)[None, None, :]
    ) & in_use[:, :, None]
    page_mine = jnp.any(match, axis=1)
    page_start = jnp.sum(jnp.where(match, slot_ids[None, :, None] * page_size, 0), axis=1)
    token_pos = page_start[:, :, None] + jnp.arange(page_size, dtype=jnp.int32)[None, None, :]
    valid = (page_mine[:, :, None] & (token_pos < lengths[:, None, None])).reshape(
        req_count, token_count
    )
    keys = k_pool.reshape(token_count, kv_local, head_dim)
    values = v_pool.reshape(token_count, kv_local, head_dim)
    scores = (
        jnp.einsum("rkgd,tkd->rkgt", queries, keys, preferred_element_type=jnp.float32)
        * score_scale
    )
    scores = jnp.where(valid[:, None, None, :], scores, -jnp.inf)
    own_score = (
        jnp.einsum("rkgd,rkd->rkg", queries, new_keys, preferred_element_type=jnp.float32)
        * score_scale
    )
    row_top = jnp.maximum(jnp.max(scores, axis=-1), own_score)
    exps_all = jnp.exp(scores - row_top[..., None])
    own_exp = jnp.exp(own_score - row_top)
    denom_sum = jnp.sum(exps_all, axis=-1) + own_exp
    weights = (exps_all / denom_sum[..., None]).astype(jnp.bfloat16)
    own_weight = (own_exp / denom_sum).astype(jnp.bfloat16)
    start_sum = jnp.einsum(
        "rkg,rkd->rkgd", own_weight, new_values, preferred_element_type=jnp.float32
    )
    return start_sum + jnp.einsum(
        "rkgt,tkd->rkgd", weights, values, preferred_element_type=jnp.float32
    )


def reduce_to_slice(partial, kv_count, slice_width):
    rows = partial.shape[0]
    pieces = partial.reshape(rows, kv_count, slice_width).transpose(1, 0, 2)
    arrived = lax.all_to_all(pieces, "kv", 0, 0, tiled=True)
    return jnp.sum(arrived, axis=0)


def layer_body(
    hidden,
    attn_gain,
    q_gain,
    k_gain,
    w_q,
    w_gate_attn,
    w_k,
    w_v,
    w_o,
    k_pool,
    v_pool,
    lengths,
    page_table,
    mig_request,
    mig_dest,
    mlp_gain,
    w_gate,
    w_up,
    w_down,
):
    head_dim = q_gain.shape[0]
    req_count = hidden.shape[0]
    kv_local = w_k.shape[1] // head_dim
    q_local = w_q.shape[1] // head_dim
    group_size = q_local // kv_local
    page_size = k_pool.shape[1]
    channels = kv_local * head_dim
    model_width = mlp_gain.shape[0]
    unit_count = w_gate.shape[1]
    stacked = lax.all_gather(
        jnp.concatenate([w_gate.T, w_up.T, w_down.T], axis=0), "req", axis=0, tiled=False
    )
    gate_w = stacked[:, :unit_count, :]
    up_w = stacked[:, unit_count : 2 * unit_count, :]
    down_w = stacked[:, 2 * unit_count :, :]
    whole_rows = lax.all_gather(hidden, "kv", axis=1, tiled=True)
    normed = rms_norm(whole_rows, attn_gain).astype(jnp.bfloat16)
    query_raw = jnp.dot(normed, w_q, preferred_element_type=jnp.float32).reshape(
        req_count, q_local, head_dim
    )
    gate_raw = jnp.dot(normed, w_gate_attn, preferred_element_type=jnp.float32)
    key_raw = jnp.dot(normed, w_k, preferred_element_type=jnp.float32).reshape(
        req_count, kv_local, head_dim
    )
    value_raw = jnp.dot(normed, w_v, preferred_element_type=jnp.float32).reshape(
        req_count, kv_local, head_dim
    )
    queries = rotate(rms_norm(query_raw, q_gain), lengths).astype(jnp.bfloat16)
    queries = queries.reshape(req_count, kv_local, group_size, head_dim)
    new_keys = rotate(rms_norm(key_raw, k_gain), lengths).astype(jnp.bfloat16)
    new_values = value_raw.astype(jnp.bfloat16)
    mig_rows = mig_request[0]
    dest_row = mig_dest[0]
    mig_count = mig_rows.shape[0]
    slot_count = MIGP * page_size
    inverse = jnp.zeros_like(dest_row).at[dest_row].set(jnp.arange(mig_count, dtype=jnp.int32))
    sent_rows = mig_rows[inverse]
    moved_pages = page_table[sent_rows, :MIGP]
    slot_pos = jnp.arange(slot_count, dtype=jnp.int32)[None, :, None]
    moved_len = lengths[sent_rows][:, None, None]
    zero_value = jnp.zeros((), jnp.bfloat16)

    def place_cache(pool, fresh_rows):
        cached = pool[moved_pages].reshape(mig_count, slot_count, channels)
        fresh_row = fresh_rows.reshape(req_count, channels)[sent_rows][:, None, :]
        return jnp.where(
            slot_pos < moved_len, cached, jnp.where(slot_pos == moved_len, fresh_row, zero_value)
        )

    moving = lax.all_to_all(
        jnp.stack([place_cache(k_pool, new_keys), place_cache(v_pool, new_values)], axis=1),
        "req",
        0,
        0,
        tiled=True,
    )
    mig_keys = moving[:, 0]
    mig_values = moving[:, 1]
    context = attend_pool(queries, new_keys, new_values, k_pool, v_pool, lengths, page_table)
    gated = (jax.nn.sigmoid(gate_raw) * context.reshape(req_count, q_local * head_dim)).astype(
        jnp.bfloat16
    )
    head_terms = jnp.dot(gated, w_o, preferred_element_type=jnp.float32)
    kv_count = lax.axis_size("kv")
    slice_width = model_width // kv_count
    mid_slice = (
        hidden.astype(jnp.float32) + reduce_to_slice(head_terms, kv_count, slice_width)
    ).astype(jnp.bfloat16)
    mid_stream = lax.all_gather(mid_slice, "kv", axis=1, tiled=True)
    normed_mlp = rms_norm(mid_stream, mlp_gain).astype(jnp.bfloat16)
    gate_part = jnp.einsum("rd,sud->rsu", normed_mlp, gate_w, preferred_element_type=jnp.float32)
    up_part = jnp.einsum("rd,sud->rsu", normed_mlp, up_w, preferred_element_type=jnp.float32)
    activation = (jax.nn.silu(gate_part) * up_part).astype(jnp.bfloat16)
    down_part = jnp.einsum(
        "rsu,suc->rc", activation, down_w, preferred_element_type=jnp.float32
    )
    mlp_part = reduce_to_slice(down_part, kv_count, slice_width)
    out_hidden = (mid_slice.astype(jnp.float32) + mlp_part).astype(jnp.bfloat16)
    return (out_hidden, mig_keys, mig_values)


def solution(mesh):
    return jax.shard_map(
        layer_body,
        mesh=mesh,
        in_specs=(
            P("req", "kv"),
            P(),
            P(),
            P(),
            P(None, "kv"),
            P(None, "kv"),
            P(None, "kv"),
            P(None, "kv"),
            P("kv", None),
            P("req", None, "kv"),
            P("req", None, "kv"),
            P("req"),
            P("req", None),
            P("req", None),
            P("req", None),
            P(),
            P(None, ("req", "kv")),
            P(None, ("req", "kv")),
            P(None, ("req", "kv")),
        ),
        out_specs=(P("req", "kv"), P("req", None, "kv"), P("req", None, "kv")),
        check_vma=False,
    )
```

```python
import jax
import jax.numpy as jnp
from jax import lax
from jax.sharding import PartitionSpec as P

MIGP = 4


EPSILON = 1e-06
ROPE_BASE = 1000000.0


def rms_norm(values, scale_row):
    values = values.astype(jnp.float32)
    return (
        values * lax.rsqrt(jnp.mean(values * values, axis=-1, keepdims=True) + EPSILON) * scale_row
    )


def rotate(values, position):
    half_dim = values.shape[-1] // 2
    frequency = ROPE_BASE ** (-jnp.arange(half_dim, dtype=jnp.float32) * 2.0 / values.shape[-1])
    angles = position.astype(jnp.float32)[:, None, None] * frequency
    cosine = jnp.cos(angles)
    sine_part = jnp.sin(angles)
    first_half = values[..., :half_dim]
    second = values[..., half_dim:]
    return jnp.concatenate(
        [first_half * cosine - second * sine_part, second * cosine + first_half * sine_part],
        axis=-1,
    )


def attend_pool(queries, new_keys, new_values, k_pool, v_pool, lengths, page_table):
    req_count, kv_local, _, head_dim = queries.shape
    pool_pages, page_size, _ = k_pool.shape
    table_width = page_table.shape[1]
    token_count = pool_pages * page_size
    score_scale = head_dim ** (-0.5)
    slot_ids = jnp.arange(table_width, dtype=jnp.int32)
    in_use = slot_ids[None, :] < (lengths // page_size + 1)[:, None]
    match = (
        page_table[:, :, None] == jnp.arange(pool_pages, dtype=jnp.int32)[None, None, :]
    ) & in_use[:, :, None]
    page_mine = jnp.any(match, axis=1)
    page_start = jnp.sum(jnp.where(match, slot_ids[None, :, None] * page_size, 0), axis=1)
    token_pos = page_start[:, :, None] + jnp.arange(page_size, dtype=jnp.int32)[None, None, :]
    valid = (page_mine[:, :, None] & (token_pos < lengths[:, None, None])).reshape(
        req_count, token_count
    )
    keys = k_pool.reshape(token_count, kv_local, head_dim)
    values = v_pool.reshape(token_count, kv_local, head_dim)
    scores = (
        jnp.einsum("rkgd,tkd->rkgt", queries, keys, preferred_element_type=jnp.float32)
        * score_scale
    )
    scores = jnp.where(valid[:, None, None, :], scores, -jnp.inf)
    own_score = (
        jnp.einsum("rkgd,rkd->rkg", queries, new_keys, preferred_element_type=jnp.float32)
        * score_scale
    )
    row_top = jnp.maximum(jnp.max(scores, axis=-1), own_score)
    exps_all = jnp.exp(scores - row_top[..., None])
    own_exp = jnp.exp(own_score - row_top)
    denom_sum = jnp.sum(exps_all, axis=-1) + own_exp
    weights = (exps_all / denom_sum[..., None]).astype(jnp.bfloat16)
    own_weight = (own_exp / denom_sum).astype(jnp.bfloat16)
    start_sum = jnp.einsum(
        "rkg,rkd->rkgd", own_weight, new_values, preferred_element_type=jnp.float32
    )
    return start_sum + jnp.einsum(
        "rkgt,tkd->rkgd", weights, values, preferred_element_type=jnp.float32
    )


def reduce_to_slice(partial, kv_count, slice_width):
    rows = partial.shape[0]
    pieces = partial.reshape(rows, kv_count, slice_width).transpose(1, 0, 2)
    arrived = lax.all_to_all(pieces, "kv", 0, 0, tiled=True)
    return jnp.sum(arrived, axis=0)


def layer_body(
    hidden,
    attn_gain,
    q_gain,
    k_gain,
    w_q,
    w_gate_attn,
    w_k,
    w_v,
    w_o,
    k_pool,
    v_pool,
    lengths,
    page_table,
    mig_request,
    mig_dest,
    mlp_gain,
    w_gate,
    w_up,
    w_down,
):
    head_dim = q_gain.shape[0]
    req_count = hidden.shape[0]
    kv_local = w_k.shape[1] // head_dim
    q_local = w_q.shape[1] // head_dim
    group_size = q_local // kv_local
    page_size = k_pool.shape[1]
    channels = kv_local * head_dim
    model_width = mlp_gain.shape[0]
    unit_count = w_gate.shape[1]
    stacked = lax.all_gather(
        jnp.concatenate([w_gate.T, w_up.T, w_down.T], axis=0), "req", axis=0, tiled=False
    )
    gate_w = stacked[:, :unit_count, :]
    up_w = stacked[:, unit_count : 2 * unit_count, :]
    down_w = stacked[:, 2 * unit_count :, :]
    whole_rows = lax.all_gather(hidden, "kv", axis=1, tiled=True)
    normed = rms_norm(whole_rows, attn_gain).astype(jnp.bfloat16)
    query_raw = jnp.dot(normed, w_q, preferred_element_type=jnp.float32).reshape(
        req_count, q_local, head_dim
    )
    gate_raw = jnp.dot(normed, w_gate_attn, preferred_element_type=jnp.float32)
    key_raw = jnp.dot(normed, w_k, preferred_element_type=jnp.float32).reshape(
        req_count, kv_local, head_dim
    )
    value_raw = jnp.dot(normed, w_v, preferred_element_type=jnp.float32).reshape(
        req_count, kv_local, head_dim
    )
    queries = rotate(rms_norm(query_raw, q_gain), lengths).astype(jnp.bfloat16)
    queries = queries.reshape(req_count, kv_local, group_size, head_dim)
    new_keys = rotate(rms_norm(key_raw, k_gain), lengths).astype(jnp.bfloat16)
    new_values = value_raw.astype(jnp.bfloat16)
    mig_rows = mig_request[0]
    dest_row = mig_dest[0]
    mig_count = mig_rows.shape[0]
    slot_count = MIGP * page_size
    inverse = jnp.zeros_like(dest_row).at[dest_row].set(jnp.arange(mig_count, dtype=jnp.int32))
    sent_rows = mig_rows[inverse]
    moved_pages = page_table[sent_rows, :MIGP]
    slot_pos = jnp.arange(slot_count, dtype=jnp.int32)[None, :, None]
    moved_len = lengths[sent_rows][:, None, None]
    zero_value = jnp.zeros((), jnp.bfloat16)

    def place_cache(pool, fresh_rows):
        cached = pool[moved_pages].reshape(mig_count, slot_count, channels)
        fresh_row = fresh_rows.reshape(req_count, channels)[sent_rows][:, None, :]
        return jnp.where(
            slot_pos < moved_len, cached, jnp.where(slot_pos == moved_len, fresh_row, zero_value)
        )

    payload = jnp.stack(
        [place_cache(k_pool, new_keys), place_cache(v_pool, new_values)], axis=1
    )
    req_groups = lax.axis_size("req")
    me = lax.axis_index("req")
    arrived = [payload[me]]
    for shift in range(1, req_groups):
        arrived.append(
            lax.ppermute(
                payload[(me + shift) % req_groups],
                "req",
                [(s, (s + shift) % req_groups) for s in range(req_groups)],
            )
        )
    by_shift = jnp.stack(arrived, axis=0)
    moving = by_shift[(me - jnp.arange(req_groups, dtype=jnp.int32)) % req_groups]
    mig_keys = moving[:, 0]
    mig_values = moving[:, 1]
    context = attend_pool(queries, new_keys, new_values, k_pool, v_pool, lengths, page_table)
    gated = (jax.nn.sigmoid(gate_raw) * context.reshape(req_count, q_local * head_dim)).astype(
        jnp.bfloat16
    )
    head_terms = jnp.dot(gated, w_o, preferred_element_type=jnp.float32)
    kv_count = lax.axis_size("kv")
    slice_width = model_width // kv_count
    mid_slice = (
        hidden.astype(jnp.float32) + reduce_to_slice(head_terms, kv_count, slice_width)
    ).astype(jnp.bfloat16)
    mid_stream = lax.all_gather(mid_slice, "kv", axis=1, tiled=True)
    normed_mlp = rms_norm(mid_stream, mlp_gain).astype(jnp.bfloat16)
    gate_part = jnp.einsum("rd,sud->rsu", normed_mlp, gate_w, preferred_element_type=jnp.float32)
    up_part = jnp.einsum("rd,sud->rsu", normed_mlp, up_w, preferred_element_type=jnp.float32)
    activation = (jax.nn.silu(gate_part) * up_part).astype(jnp.bfloat16)
    down_part = jnp.einsum(
        "rsu,suc->rc", activation, down_w, preferred_element_type=jnp.float32
    )
    mlp_part = reduce_to_slice(down_part, kv_count, slice_width)
    out_hidden = (mid_slice.astype(jnp.float32) + mlp_part).astype(jnp.bfloat16)
    return (out_hidden, mig_keys, mig_values)


def solution(mesh):
    return jax.shard_map(
        layer_body,
        mesh=mesh,
        in_specs=(
            P("req", "kv"),
            P(),
            P(),
            P(),
            P(None, "kv"),
            P(None, "kv"),
            P(None, "kv"),
            P(None, "kv"),
            P("kv", None),
            P("req", None, "kv"),
            P("req", None, "kv"),
            P("req"),
            P("req", None),
            P("req", None),
            P("req", None),
            P(),
            P(None, ("req", "kv")),
            P(None, ("req", "kv")),
            P(None, ("req", "kv")),
        ),
        out_specs=(P("req", "kv"), P("req", None, "kv"), P("req", None, "kv")),
        check_vma=False,
    )
```

```python
import jax
import jax.numpy as jnp
from jax import lax
from jax.sharding import PartitionSpec as P

MIGP = 4


EPSILON = 1e-06
ROPE_BASE = 1000000.0


def rms_norm(values, scale_row):
    values = values.astype(jnp.float32)
    return (
        values * lax.rsqrt(jnp.mean(values * values, axis=-1, keepdims=True) + EPSILON) * scale_row
    )


def rotate(values, position):
    half_dim = values.shape[-1] // 2
    frequency = ROPE_BASE ** (-jnp.arange(half_dim, dtype=jnp.float32) * 2.0 / values.shape[-1])
    angles = position.astype(jnp.float32)[:, None, None] * frequency
    cosine = jnp.cos(angles)
    sine_part = jnp.sin(angles)
    first_half = values[..., :half_dim]
    second = values[..., half_dim:]
    return jnp.concatenate(
        [first_half * cosine - second * sine_part, second * cosine + first_half * sine_part],
        axis=-1,
    )


def attend_pool(queries, new_keys, new_values, k_pool, v_pool, lengths, page_table):
    req_count, kv_local, _, head_dim = queries.shape
    pool_pages, page_size, _ = k_pool.shape
    table_width = page_table.shape[1]
    token_count = pool_pages * page_size
    score_scale = head_dim ** (-0.5)
    slot_ids = jnp.arange(table_width, dtype=jnp.int32)
    in_use = slot_ids[None, :] < (lengths // page_size + 1)[:, None]
    match = (
        page_table[:, :, None] == jnp.arange(pool_pages, dtype=jnp.int32)[None, None, :]
    ) & in_use[:, :, None]
    page_mine = jnp.any(match, axis=1)
    page_start = jnp.sum(jnp.where(match, slot_ids[None, :, None] * page_size, 0), axis=1)
    token_pos = page_start[:, :, None] + jnp.arange(page_size, dtype=jnp.int32)[None, None, :]
    valid = (page_mine[:, :, None] & (token_pos < lengths[:, None, None])).reshape(
        req_count, token_count
    )
    keys = k_pool.reshape(token_count, kv_local, head_dim)
    values = v_pool.reshape(token_count, kv_local, head_dim)
    scores = (
        jnp.einsum("rkgd,tkd->rkgt", queries, keys, preferred_element_type=jnp.float32)
        * score_scale
    )
    scores = jnp.where(valid[:, None, None, :], scores, -jnp.inf)
    own_score = (
        jnp.einsum("rkgd,rkd->rkg", queries, new_keys, preferred_element_type=jnp.float32)
        * score_scale
    )
    row_top = jnp.maximum(jnp.max(scores, axis=-1), own_score)
    exps_all = jnp.exp(scores - row_top[..., None])
    own_exp = jnp.exp(own_score - row_top)
    denom_sum = jnp.sum(exps_all, axis=-1) + own_exp
    weights = (exps_all / denom_sum[..., None]).astype(jnp.bfloat16)
    own_weight = (own_exp / denom_sum).astype(jnp.bfloat16)
    start_sum = jnp.einsum(
        "rkg,rkd->rkgd", own_weight, new_values, preferred_element_type=jnp.float32
    )
    return start_sum + jnp.einsum(
        "rkgt,tkd->rkgd", weights, values, preferred_element_type=jnp.float32
    )


def reduce_to_slice(partial, kv_count, slice_width):
    rows = partial.shape[0]
    pieces = partial.reshape(rows, kv_count, slice_width).transpose(1, 0, 2)
    arrived = lax.all_to_all(pieces, "kv", 0, 0, tiled=True)
    return jnp.sum(arrived, axis=0)


def layer_body(
    hidden,
    attn_gain,
    q_gain,
    k_gain,
    w_q,
    w_gate_attn,
    w_k,
    w_v,
    w_o,
    k_pool,
    v_pool,
    lengths,
    page_table,
    mig_request,
    mig_dest,
    mlp_gain,
    w_gate,
    w_up,
    w_down,
):
    head_dim = q_gain.shape[0]
    req_count = hidden.shape[0]
    kv_local = w_k.shape[1] // head_dim
    q_local = w_q.shape[1] // head_dim
    group_size = q_local // kv_local
    page_size = k_pool.shape[1]
    channels = kv_local * head_dim
    model_width = mlp_gain.shape[0]
    unit_count = w_gate.shape[1]
    stacked = lax.all_gather(
        jnp.concatenate([w_gate.T, w_up.T, w_down.T], axis=0), "req", axis=0, tiled=False
    )
    gate_w = stacked[:, :unit_count, :]
    up_w = stacked[:, unit_count : 2 * unit_count, :]
    down_w = stacked[:, 2 * unit_count :, :]
    kv_count = lax.axis_size("kv")
    whole_rows = (
        lax.all_to_all(
            jnp.broadcast_to(hidden[None], (kv_count,) + hidden.shape), "kv", 0, 0, tiled=True
        )
        .transpose(1, 0, 2)
        .reshape(req_count, kv_count * hidden.shape[1])
    )
    normed = rms_norm(whole_rows, attn_gain).astype(jnp.bfloat16)
    query_raw = jnp.dot(normed, w_q, preferred_element_type=jnp.float32).reshape(
        req_count, q_local, head_dim
    )
    gate_raw = jnp.dot(normed, w_gate_attn, preferred_element_type=jnp.float32)
    key_raw = jnp.dot(normed, w_k, preferred_element_type=jnp.float32).reshape(
        req_count, kv_local, head_dim
    )
    value_raw = jnp.dot(normed, w_v, preferred_element_type=jnp.float32).reshape(
        req_count, kv_local, head_dim
    )
    queries = rotate(rms_norm(query_raw, q_gain), lengths).astype(jnp.bfloat16)
    queries = queries.reshape(req_count, kv_local, group_size, head_dim)
    new_keys = rotate(rms_norm(key_raw, k_gain), lengths).astype(jnp.bfloat16)
    new_values = value_raw.astype(jnp.bfloat16)
    mig_rows = mig_request[0]
    dest_row = mig_dest[0]
    mig_count = mig_rows.shape[0]
    slot_count = MIGP * page_size
    inverse = jnp.zeros_like(dest_row).at[dest_row].set(jnp.arange(mig_count, dtype=jnp.int32))
    sent_rows = mig_rows[inverse]
    moved_pages = page_table[sent_rows, :MIGP]
    slot_pos = jnp.arange(slot_count, dtype=jnp.int32)[None, :, None]
    moved_len = lengths[sent_rows][:, None, None]
    zero_value = jnp.zeros((), jnp.bfloat16)

    cached_pages = lax.optimization_barrier((k_pool[moved_pages], v_pool[moved_pages]))

    def place_cache(pool_pages, fresh_rows):
        cached = pool_pages.reshape(mig_count, slot_count, channels)
        fresh_row = fresh_rows.reshape(req_count, channels)[sent_rows][:, None, :]
        return jnp.where(
            slot_pos < moved_len, cached, jnp.where(slot_pos == moved_len, fresh_row, zero_value)
        )

    moving = lax.all_to_all(
        jnp.stack([place_cache(cached_pages[0], new_keys), place_cache(cached_pages[1], new_values)], axis=1),
        "req",
        0,
        0,
        tiled=True,
    )
    mig_keys = moving[:, 0]
    mig_values = moving[:, 1]
    context = attend_pool(queries, new_keys, new_values, k_pool, v_pool, lengths, page_table)
    gated = (jax.nn.sigmoid(gate_raw) * context.reshape(req_count, q_local * head_dim)).astype(
        jnp.bfloat16
    )
    head_terms = jnp.dot(gated, w_o, preferred_element_type=jnp.float32)
    slice_width = model_width // kv_count
    mid_slice = (
        hidden.astype(jnp.float32) + reduce_to_slice(head_terms, kv_count, slice_width)
    ).astype(jnp.bfloat16)
    mid_stream = lax.all_gather(mid_slice, "kv", axis=1, tiled=True)
    normed_mlp = rms_norm(mid_stream, mlp_gain).astype(jnp.bfloat16)
    gate_part = jnp.einsum("rd,sud->rsu", normed_mlp, gate_w, preferred_element_type=jnp.float32)
    up_part = jnp.einsum("rd,sud->rsu", normed_mlp, up_w, preferred_element_type=jnp.float32)
    activation = (jax.nn.silu(gate_part) * up_part).astype(jnp.bfloat16)
    down_part = jnp.einsum(
        "rsu,suc->rc", activation, down_w, preferred_element_type=jnp.float32
    )
    mlp_part = reduce_to_slice(down_part, kv_count, slice_width)
    out_hidden = (mid_slice.astype(jnp.float32) + mlp_part).astype(jnp.bfloat16)
    return (out_hidden, mig_keys, mig_values)


def solution(mesh):
    return jax.shard_map(
        layer_body,
        mesh=mesh,
        in_specs=(
            P("req", "kv"),
            P(),
            P(),
            P(),
            P(None, "kv"),
            P(None, "kv"),
            P(None, "kv"),
            P(None, "kv"),
            P("kv", None),
            P("req", None, "kv"),
            P("req", None, "kv"),
            P("req"),
            P("req", None),
            P("req", None),
            P("req", None),
            P(),
            P(None, ("req", "kv")),
            P(None, ("req", "kv")),
            P(None, ("req", "kv")),
        ),
        out_specs=(P("req", "kv"), P("req", None, "kv"), P("req", None, "kv")),
        check_vma=False,
    )
```

```python
import jax
import jax.numpy as jnp
from jax import lax
from jax.sharding import PartitionSpec as P

MIGP = 4


EPSILON = 1e-06
ROPE_BASE = 1000000.0


def rms_norm(values, scale_row):
    values = values.astype(jnp.float32)
    return (
        values * lax.rsqrt(jnp.mean(values * values, axis=-1, keepdims=True) + EPSILON) * scale_row
    )


def rotate(values, position):
    half_dim = values.shape[-1] // 2
    frequency = ROPE_BASE ** (-jnp.arange(half_dim, dtype=jnp.float32) * 2.0 / values.shape[-1])
    angles = position.astype(jnp.float32)[:, None, None] * frequency
    cosine = jnp.cos(angles)
    sine_part = jnp.sin(angles)
    first_half = values[..., :half_dim]
    second = values[..., half_dim:]
    return jnp.concatenate(
        [first_half * cosine - second * sine_part, second * cosine + first_half * sine_part],
        axis=-1,
    )


def attend_pool(queries, new_keys, new_values, k_pool, v_pool, lengths, page_table):
    req_count, kv_local, _, head_dim = queries.shape
    pool_pages, page_size, _ = k_pool.shape
    table_width = page_table.shape[1]
    token_count = pool_pages * page_size
    score_scale = head_dim ** (-0.5)
    slot_ids = jnp.arange(table_width, dtype=jnp.int32)
    in_use = slot_ids[None, :] < (lengths // page_size + 1)[:, None]
    match = (
        page_table[:, :, None] == jnp.arange(pool_pages, dtype=jnp.int32)[None, None, :]
    ) & in_use[:, :, None]
    page_mine = jnp.any(match, axis=1)
    page_start = jnp.sum(jnp.where(match, slot_ids[None, :, None] * page_size, 0), axis=1)
    token_pos = page_start[:, :, None] + jnp.arange(page_size, dtype=jnp.int32)[None, None, :]
    valid = (page_mine[:, :, None] & (token_pos < lengths[:, None, None])).reshape(
        req_count, token_count
    )
    keys = k_pool.reshape(token_count, kv_local, head_dim)
    values = v_pool.reshape(token_count, kv_local, head_dim)
    scores = (
        jnp.einsum("rkgd,tkd->rkgt", queries, keys, preferred_element_type=jnp.float32)
        * score_scale
    )
    scores = jnp.where(valid[:, None, None, :], scores, -jnp.inf)
    own_score = (
        jnp.einsum("rkgd,rkd->rkg", queries, new_keys, preferred_element_type=jnp.float32)
        * score_scale
    )
    row_top = jnp.maximum(jnp.max(scores, axis=-1), own_score)
    exps_all = jnp.exp(scores - row_top[..., None])
    own_exp = jnp.exp(own_score - row_top)
    denom_sum = jnp.sum(exps_all, axis=-1) + own_exp
    weights = (exps_all / denom_sum[..., None]).astype(jnp.bfloat16)
    own_weight = (own_exp / denom_sum).astype(jnp.bfloat16)
    start_sum = jnp.einsum(
        "rkg,rkd->rkgd", own_weight, new_values, preferred_element_type=jnp.float32
    )
    return start_sum + jnp.einsum(
        "rkgt,tkd->rkgd", weights, values, preferred_element_type=jnp.float32
    )


def reduce_to_slice(partial, kv_count, slice_width):
    rows = partial.shape[0]
    pieces = partial.reshape(rows, kv_count, slice_width).transpose(1, 0, 2)
    arrived = lax.all_to_all(pieces, "kv", 0, 0, tiled=True)
    return jnp.sum(arrived, axis=0)


def reduce_by_permutes(partial, kv_count, slice_width):
    rows = partial.shape[0]
    pieces = partial.reshape(rows, kv_count, slice_width).transpose(1, 0, 2)
    me = lax.axis_index("kv")
    total = pieces[me]
    for shift in range(1, kv_count):
        total = total + lax.ppermute(
            pieces[(me + shift) % kv_count],
            "kv",
            [(k, (k + shift) % kv_count) for k in range(kv_count)],
        )
    return total


def layer_body(
    hidden,
    attn_gain,
    q_gain,
    k_gain,
    w_q,
    w_gate_attn,
    w_k,
    w_v,
    w_o,
    k_pool,
    v_pool,
    lengths,
    page_table,
    mig_request,
    mig_dest,
    mlp_gain,
    w_gate,
    w_up,
    w_down,
):
    head_dim = q_gain.shape[0]
    req_count = hidden.shape[0]
    kv_local = w_k.shape[1] // head_dim
    q_local = w_q.shape[1] // head_dim
    group_size = q_local // kv_local
    page_size = k_pool.shape[1]
    channels = kv_local * head_dim
    model_width = mlp_gain.shape[0]
    unit_count = w_gate.shape[1]
    stacked = lax.all_gather(
        jnp.concatenate([w_gate.T, w_up.T, w_down.T], axis=0), "req", axis=0, tiled=False
    )
    gate_w = stacked[:, :unit_count, :]
    up_w = stacked[:, unit_count : 2 * unit_count, :]
    down_w = stacked[:, 2 * unit_count :, :]
    whole_rows = lax.all_gather(hidden, "kv", axis=1, tiled=True)
    normed = rms_norm(whole_rows, attn_gain).astype(jnp.bfloat16)
    query_raw = jnp.dot(normed, w_q, preferred_element_type=jnp.float32).reshape(
        req_count, q_local, head_dim
    )
    gate_raw = jnp.dot(normed, w_gate_attn, preferred_element_type=jnp.float32)
    key_raw = jnp.dot(normed, w_k, preferred_element_type=jnp.float32).reshape(
        req_count, kv_local, head_dim
    )
    value_raw = jnp.dot(normed, w_v, preferred_element_type=jnp.float32).reshape(
        req_count, kv_local, head_dim
    )
    queries = rotate(rms_norm(query_raw, q_gain), lengths).astype(jnp.bfloat16)
    queries = queries.reshape(req_count, kv_local, group_size, head_dim)
    new_keys = rotate(rms_norm(key_raw, k_gain), lengths).astype(jnp.bfloat16)
    new_values = value_raw.astype(jnp.bfloat16)
    mig_rows = mig_request[0]
    dest_row = mig_dest[0]
    mig_count = mig_rows.shape[0]
    slot_count = MIGP * page_size
    inverse = jnp.zeros_like(dest_row).at[dest_row].set(jnp.arange(mig_count, dtype=jnp.int32))
    sent_rows = mig_rows[inverse]
    moved_pages = page_table[sent_rows, :MIGP]
    slot_pos = jnp.arange(slot_count, dtype=jnp.int32)[None, :, None]
    moved_len = lengths[sent_rows][:, None, None]
    zero_value = jnp.zeros((), jnp.bfloat16)

    def place_cache(pool, fresh_rows):
        cached = pool[moved_pages].reshape(mig_count, slot_count, channels)
        fresh_row = fresh_rows.reshape(req_count, channels)[sent_rows][:, None, :]
        return jnp.where(
            slot_pos < moved_len, cached, jnp.where(slot_pos == moved_len, fresh_row, zero_value)
        )

    moving = lax.all_to_all(
        jnp.stack([place_cache(k_pool, new_keys), place_cache(v_pool, new_values)], axis=1),
        "req",
        0,
        0,
        tiled=True,
    )
    mig_keys = moving[:, 0]
    mig_values = moving[:, 1]
    context = attend_pool(queries, new_keys, new_values, k_pool, v_pool, lengths, page_table)
    gated = (jax.nn.sigmoid(gate_raw) * context.reshape(req_count, q_local * head_dim)).astype(
        jnp.bfloat16
    )
    head_terms = jnp.dot(gated, w_o, preferred_element_type=jnp.float32)
    kv_count = lax.axis_size("kv")
    slice_width = model_width // kv_count
    mid_slice = (
        hidden.astype(jnp.float32) + reduce_to_slice(head_terms, kv_count, slice_width)
    ).astype(jnp.bfloat16)
    mid_stream = lax.all_gather(mid_slice, "kv", axis=1, tiled=True)
    normed_mlp = rms_norm(mid_stream, mlp_gain).astype(jnp.bfloat16)
    gate_part = jnp.einsum("rd,sud->rsu", normed_mlp, gate_w, preferred_element_type=jnp.float32)
    up_part = jnp.einsum("rd,sud->rsu", normed_mlp, up_w, preferred_element_type=jnp.float32)
    activation = (jax.nn.silu(gate_part) * up_part).astype(jnp.bfloat16)
    down_part = jnp.einsum(
        "rsu,suc->rc", activation, down_w, preferred_element_type=jnp.float32
    )
    mlp_part = reduce_by_permutes(down_part, kv_count, slice_width)
    out_hidden = (mid_slice.astype(jnp.float32) + mlp_part).astype(jnp.bfloat16)
    return (out_hidden, mig_keys, mig_values)


def solution(mesh):
    return jax.shard_map(
        layer_body,
        mesh=mesh,
        in_specs=(
            P("req", "kv"),
            P(),
            P(),
            P(),
            P(None, "kv"),
            P(None, "kv"),
            P(None, "kv"),
            P(None, "kv"),
            P("kv", None),
            P("req", None, "kv"),
            P("req", None, "kv"),
            P("req"),
            P("req", None),
            P("req", None),
            P("req", None),
            P(),
            P(None, ("req", "kv")),
            P(None, ("req", "kv")),
            P(None, ("req", "kv")),
        ),
        out_specs=(P("req", "kv"), P("req", None, "kv"), P("req", None, "kv")),
        check_vma=False,
    )
```

```python
import jax
import jax.numpy as jnp
from jax import lax
from jax.sharding import PartitionSpec as P

MIGP = 4


EPSILON = 1e-06
ROPE_BASE = 1000000.0


def rms_norm(values, scale_row):
    values = values.astype(jnp.float32)
    return (
        values * lax.rsqrt(jnp.mean(values * values, axis=-1, keepdims=True) + EPSILON) * scale_row
    )


def rotate(values, position):
    half_dim = values.shape[-1] // 2
    frequency = ROPE_BASE ** (-jnp.arange(half_dim, dtype=jnp.float32) * 2.0 / values.shape[-1])
    angles = position.astype(jnp.float32)[:, None, None] * frequency
    cosine = jnp.cos(angles)
    sine_part = jnp.sin(angles)
    first_half = values[..., :half_dim]
    second = values[..., half_dim:]
    return jnp.concatenate(
        [first_half * cosine - second * sine_part, second * cosine + first_half * sine_part],
        axis=-1,
    )


def attend_pool(queries, new_keys, new_values, k_pool, v_pool, lengths, page_table):
    req_count, kv_local, _, head_dim = queries.shape
    pool_pages, page_size, _ = k_pool.shape
    table_width = page_table.shape[1]
    token_count = pool_pages * page_size
    score_scale = head_dim ** (-0.5)
    slot_ids = jnp.arange(table_width, dtype=jnp.int32)
    in_use = slot_ids[None, :] < (lengths // page_size + 1)[:, None]
    match = (
        page_table[:, :, None] == jnp.arange(pool_pages, dtype=jnp.int32)[None, None, :]
    ) & in_use[:, :, None]
    page_mine = jnp.any(match, axis=1)
    page_start = jnp.sum(jnp.where(match, slot_ids[None, :, None] * page_size, 0), axis=1)
    token_pos = page_start[:, :, None] + jnp.arange(page_size, dtype=jnp.int32)[None, None, :]
    valid = (page_mine[:, :, None] & (token_pos < lengths[:, None, None])).reshape(
        req_count, token_count
    )
    keys = k_pool.reshape(token_count, kv_local, head_dim)
    values = v_pool.reshape(token_count, kv_local, head_dim)
    scores = (
        jnp.einsum("rkgd,tkd->rkgt", queries, keys, preferred_element_type=jnp.float32)
        * score_scale
    )
    scores = jnp.where(valid[:, None, None, :], scores, -jnp.inf)
    own_score = (
        jnp.einsum("rkgd,rkd->rkg", queries, new_keys, preferred_element_type=jnp.float32)
        * score_scale
    )
    row_top = jnp.maximum(jnp.max(scores, axis=-1), own_score)
    exps_all = jnp.exp(scores - row_top[..., None])
    own_exp = jnp.exp(own_score - row_top)
    denom_sum = jnp.sum(exps_all, axis=-1) + own_exp
    weights = (exps_all / denom_sum[..., None]).astype(jnp.bfloat16)
    own_weight = (own_exp / denom_sum).astype(jnp.bfloat16)
    start_sum = jnp.einsum(
        "rkg,rkd->rkgd", own_weight, new_values, preferred_element_type=jnp.float32
    )
    return start_sum + jnp.einsum(
        "rkgt,tkd->rkgd", weights, values, preferred_element_type=jnp.float32
    )


def reduce_by_permutes(partial, kv_count, slice_width):
    rows = partial.shape[0]
    pieces = partial.reshape(rows, kv_count, slice_width).transpose(1, 0, 2)
    me = lax.axis_index("kv")
    total = pieces[me]
    for shift in range(1, kv_count):
        total = total + lax.ppermute(
            pieces[(me + shift) % kv_count],
            "kv",
            [(k, (k + shift) % kv_count) for k in range(kv_count)],
        )
    return total


def layer_body(
    hidden,
    attn_gain,
    q_gain,
    k_gain,
    w_q,
    w_gate_attn,
    w_k,
    w_v,
    w_o,
    k_pool,
    v_pool,
    lengths,
    page_table,
    mig_request,
    mig_dest,
    mlp_gain,
    w_gate,
    w_up,
    w_down,
):
    head_dim = q_gain.shape[0]
    req_count = hidden.shape[0]
    kv_local = w_k.shape[1] // head_dim
    q_local = w_q.shape[1] // head_dim
    group_size = q_local // kv_local
    page_size = k_pool.shape[1]
    channels = kv_local * head_dim
    model_width = mlp_gain.shape[0]
    unit_count = w_gate.shape[1]
    stacked = lax.all_gather(
        jnp.concatenate([w_gate.T, w_up.T, w_down.T], axis=0), "req", axis=0, tiled=False
    )
    gate_w = stacked[:, :unit_count, :]
    up_w = stacked[:, unit_count : 2 * unit_count, :]
    down_w = stacked[:, 2 * unit_count :, :]
    whole_rows = lax.all_gather(hidden, "kv", axis=1, tiled=True)
    normed = rms_norm(whole_rows, attn_gain).astype(jnp.bfloat16)
    query_raw = jnp.dot(normed, w_q, preferred_element_type=jnp.float32).reshape(
        req_count, q_local, head_dim
    )
    gate_raw = jnp.dot(normed, w_gate_attn, preferred_element_type=jnp.float32)
    key_raw = jnp.dot(normed, w_k, preferred_element_type=jnp.float32).reshape(
        req_count, kv_local, head_dim
    )
    value_raw = jnp.dot(normed, w_v, preferred_element_type=jnp.float32).reshape(
        req_count, kv_local, head_dim
    )
    queries = rotate(rms_norm(query_raw, q_gain), lengths).astype(jnp.bfloat16)
    queries = queries.reshape(req_count, kv_local, group_size, head_dim)
    new_keys = rotate(rms_norm(key_raw, k_gain), lengths).astype(jnp.bfloat16)
    new_values = value_raw.astype(jnp.bfloat16)
    mig_rows = mig_request[0]
    dest_row = mig_dest[0]
    mig_count = mig_rows.shape[0]
    slot_count = MIGP * page_size
    inverse = jnp.zeros_like(dest_row).at[dest_row].set(jnp.arange(mig_count, dtype=jnp.int32))
    sent_rows = mig_rows[inverse]
    moved_pages = page_table[sent_rows, :MIGP]
    slot_pos = jnp.arange(slot_count, dtype=jnp.int32)[None, :, None]
    moved_len = lengths[sent_rows][:, None, None]
    zero_value = jnp.zeros((), jnp.bfloat16)

    def place_cache(pool, fresh_rows):
        cached = pool[moved_pages].reshape(mig_count, slot_count, channels)
        fresh_row = fresh_rows.reshape(req_count, channels)[sent_rows][:, None, :]
        return jnp.where(
            slot_pos < moved_len, cached, jnp.where(slot_pos == moved_len, fresh_row, zero_value)
        )

    moving = lax.all_to_all(
        jnp.stack([place_cache(k_pool, new_keys), place_cache(v_pool, new_values)], axis=0),
        "req",
        1,
        1,
        tiled=True,
    )
    mig_keys = moving[0]
    mig_values = moving[1]
    context = attend_pool(queries, new_keys, new_values, k_pool, v_pool, lengths, page_table)
    gated = (jax.nn.sigmoid(gate_raw) * context.reshape(req_count, q_local * head_dim)).astype(
        jnp.bfloat16
    )
    head_terms = jnp.dot(gated, w_o, preferred_element_type=jnp.float32)
    kv_count = lax.axis_size("kv")
    slice_width = model_width // kv_count
    mid_slice = (
        hidden.astype(jnp.float32) + reduce_by_permutes(head_terms, kv_count, slice_width)
    ).astype(jnp.bfloat16)
    mid_stream = lax.all_gather(mid_slice, "kv", axis=1, tiled=True)
    normed_mlp = rms_norm(mid_stream, mlp_gain).astype(jnp.bfloat16)
    gate_part = jnp.einsum("rd,sud->rsu", normed_mlp, gate_w, preferred_element_type=jnp.float32)
    up_part = jnp.einsum("rd,sud->rsu", normed_mlp, up_w, preferred_element_type=jnp.float32)
    activation = (jax.nn.silu(gate_part) * up_part).astype(jnp.bfloat16)
    down_part = jnp.einsum(
        "rsu,suc->rc", activation, down_w, preferred_element_type=jnp.float32
    )
    mlp_part = reduce_by_permutes(down_part, kv_count, slice_width)
    out_hidden = (mid_slice.astype(jnp.float32) + mlp_part).astype(jnp.bfloat16)
    return (out_hidden, mig_keys, mig_values)


def solution(mesh):
    return jax.shard_map(
        layer_body,
        mesh=mesh,
        in_specs=(
            P("req", "kv"),
            P(),
            P(),
            P(),
            P(None, "kv"),
            P(None, "kv"),
            P(None, "kv"),
            P(None, "kv"),
            P("kv", None),
            P("req", None, "kv"),
            P("req", None, "kv"),
            P("req"),
            P("req", None),
            P("req", None),
            P("req", None),
            P(),
            P(None, ("req", "kv")),
            P(None, ("req", "kv")),
            P(None, ("req", "kv")),
        ),
        out_specs=(P("req", "kv"), P("req", None, "kv"), P("req", None, "kv")),
        check_vma=False,
    )
```

```python
import jax
import jax.numpy as jnp
from jax import lax
from jax.sharding import PartitionSpec as P

MIGP = 4


EPSILON = 1e-06
ROPE_BASE = 1000000.0


def rms_norm(values, scale_row):
    values = values.astype(jnp.float32)
    return (
        values * lax.rsqrt(jnp.mean(values * values, axis=-1, keepdims=True) + EPSILON) * scale_row
    )


def rotate(values, position):
    half_dim = values.shape[-1] // 2
    frequency = ROPE_BASE ** (-jnp.arange(half_dim, dtype=jnp.float32) * 2.0 / values.shape[-1])
    angles = position.astype(jnp.float32)[:, None, None] * frequency
    cosine = jnp.cos(angles)
    sine_part = jnp.sin(angles)
    first_half = values[..., :half_dim]
    second = values[..., half_dim:]
    return jnp.concatenate(
        [first_half * cosine - second * sine_part, second * cosine + first_half * sine_part],
        axis=-1,
    )


def attend_pool(queries, new_keys, new_values, k_pool, v_pool, lengths, page_table):
    req_count, kv_local, _, head_dim = queries.shape
    pool_pages, page_size, _ = k_pool.shape
    table_width = page_table.shape[1]
    token_count = pool_pages * page_size
    score_scale = head_dim ** (-0.5)
    slot_ids = jnp.arange(table_width, dtype=jnp.int32)
    in_use = slot_ids[None, :] < (lengths // page_size + 1)[:, None]
    match = (
        page_table[:, :, None] == jnp.arange(pool_pages, dtype=jnp.int32)[None, None, :]
    ) & in_use[:, :, None]
    page_mine = jnp.any(match, axis=1)
    page_start = jnp.sum(jnp.where(match, slot_ids[None, :, None] * page_size, 0), axis=1)
    token_pos = page_start[:, :, None] + jnp.arange(page_size, dtype=jnp.int32)[None, None, :]
    valid = (page_mine[:, :, None] & (token_pos < lengths[:, None, None])).reshape(
        req_count, token_count
    )
    keys = k_pool.reshape(token_count, kv_local, head_dim)
    values = v_pool.reshape(token_count, kv_local, head_dim)
    scores = (
        jnp.einsum("rkgd,tkd->rkgt", queries, keys, preferred_element_type=jnp.float32)
        * score_scale
    )
    scores = jnp.where(valid[:, None, None, :], scores, -jnp.inf)
    own_score = (
        jnp.einsum("rkgd,rkd->rkg", queries, new_keys, preferred_element_type=jnp.float32)
        * score_scale
    )
    row_top = jnp.maximum(jnp.max(scores, axis=-1), own_score)
    exps_all = jnp.exp(scores - row_top[..., None])
    own_exp = jnp.exp(own_score - row_top)
    denom_sum = jnp.sum(exps_all, axis=-1) + own_exp
    weights = (exps_all / denom_sum[..., None]).astype(jnp.bfloat16)
    own_weight = (own_exp / denom_sum).astype(jnp.bfloat16)
    start_sum = jnp.einsum(
        "rkg,rkd->rkgd", own_weight, new_values, preferred_element_type=jnp.float32
    )
    return start_sum + jnp.einsum(
        "rkgt,tkd->rkgd", weights, values, preferred_element_type=jnp.float32
    )


def reduce_by_permutes(partial, kv_count, slice_width):
    rows = partial.shape[0]
    pieces = partial.reshape(rows, kv_count, slice_width).transpose(1, 0, 2)
    me = lax.axis_index("kv")
    total = pieces[me]
    for shift in range(1, kv_count):
        total = total + lax.ppermute(
            pieces[(me + shift) % kv_count],
            "kv",
            [(k, (k + shift) % kv_count) for k in range(kv_count)],
        )
    return total


def layer_body(
    hidden,
    attn_gain,
    q_gain,
    k_gain,
    w_q,
    w_gate_attn,
    w_k,
    w_v,
    w_o,
    k_pool,
    v_pool,
    lengths,
    page_table,
    mig_request,
    mig_dest,
    mlp_gain,
    w_gate,
    w_up,
    w_down,
):
    head_dim = q_gain.shape[0]
    req_count = hidden.shape[0]
    kv_local = w_k.shape[1] // head_dim
    q_local = w_q.shape[1] // head_dim
    group_size = q_local // kv_local
    page_size = k_pool.shape[1]
    channels = kv_local * head_dim
    model_width = mlp_gain.shape[0]
    unit_count = w_gate.shape[1]
    stacked = lax.all_gather(
        jnp.concatenate([w_gate.T, w_up.T], axis=0), "req", axis=0, tiled=False
    )
    req_groups = lax.axis_size("req")
    down_w = lax.all_to_all(
        jnp.broadcast_to(w_down.T[None], (req_groups,) + w_down.T.shape),
        "req",
        0,
        0,
        tiled=True,
    )
    gate_w = stacked[:, :unit_count, :]
    up_w = stacked[:, unit_count:, :]
    whole_rows = lax.all_gather(hidden, "kv", axis=1, tiled=True)
    normed = rms_norm(whole_rows, attn_gain).astype(jnp.bfloat16)
    query_raw = jnp.dot(normed, w_q, preferred_element_type=jnp.float32).reshape(
        req_count, q_local, head_dim
    )
    gate_raw = jnp.dot(normed, w_gate_attn, preferred_element_type=jnp.float32)
    key_raw = jnp.dot(normed, w_k, preferred_element_type=jnp.float32).reshape(
        req_count, kv_local, head_dim
    )
    value_raw = jnp.dot(normed, w_v, preferred_element_type=jnp.float32).reshape(
        req_count, kv_local, head_dim
    )
    queries = rotate(rms_norm(query_raw, q_gain), lengths).astype(jnp.bfloat16)
    queries = queries.reshape(req_count, kv_local, group_size, head_dim)
    new_keys = rotate(rms_norm(key_raw, k_gain), lengths).astype(jnp.bfloat16)
    new_values = value_raw.astype(jnp.bfloat16)
    mig_rows = mig_request[0]
    dest_row = mig_dest[0]
    mig_count = mig_rows.shape[0]
    slot_count = MIGP * page_size
    inverse = jnp.zeros_like(dest_row).at[dest_row].set(jnp.arange(mig_count, dtype=jnp.int32))
    sent_rows = mig_rows[inverse]
    moved_pages = page_table[sent_rows, :MIGP]
    slot_pos = jnp.arange(slot_count, dtype=jnp.int32)[None, :, None]
    moved_len = lengths[sent_rows][:, None, None]
    zero_value = jnp.zeros((), jnp.bfloat16)

    def place_cache(pool, fresh_rows):
        cached = pool[moved_pages].reshape(mig_count, slot_count, channels)
        fresh_row = fresh_rows.reshape(req_count, channels)[sent_rows][:, None, :]
        return jnp.where(
            slot_pos < moved_len, cached, jnp.where(slot_pos == moved_len, fresh_row, zero_value)
        )

    moving = lax.all_to_all(
        jnp.stack([place_cache(k_pool, new_keys), place_cache(v_pool, new_values)], axis=1),
        "req",
        0,
        0,
        tiled=True,
    )
    mig_keys = moving[:, 0]
    mig_values = moving[:, 1]
    context = attend_pool(queries, new_keys, new_values, k_pool, v_pool, lengths, page_table)
    gated = (jax.nn.sigmoid(gate_raw) * context.reshape(req_count, q_local * head_dim)).astype(
        jnp.bfloat16
    )
    head_terms = jnp.dot(gated, w_o, preferred_element_type=jnp.float32)
    kv_count = lax.axis_size("kv")
    slice_width = model_width // kv_count
    mid_slice = (
        hidden.astype(jnp.float32) + reduce_by_permutes(head_terms, kv_count, slice_width)
    ).astype(jnp.bfloat16)
    mid_stream = lax.all_gather(mid_slice, "kv", axis=1, tiled=True)
    normed_mlp = rms_norm(mid_stream, mlp_gain).astype(jnp.bfloat16)
    gate_part = jnp.einsum("rd,sud->rsu", normed_mlp, gate_w, preferred_element_type=jnp.float32)
    up_part = jnp.einsum("rd,sud->rsu", normed_mlp, up_w, preferred_element_type=jnp.float32)
    activation = (jax.nn.silu(gate_part) * up_part).astype(jnp.bfloat16)
    down_part = jnp.einsum(
        "rsu,suc->rc", activation, down_w, preferred_element_type=jnp.float32
    )
    mlp_part = reduce_by_permutes(down_part, kv_count, slice_width)
    out_hidden = (mid_slice.astype(jnp.float32) + mlp_part).astype(jnp.bfloat16)
    return (out_hidden, mig_keys, mig_values)


def solution(mesh):
    return jax.shard_map(
        layer_body,
        mesh=mesh,
        in_specs=(
            P("req", "kv"),
            P(),
            P(),
            P(),
            P(None, "kv"),
            P(None, "kv"),
            P(None, "kv"),
            P(None, "kv"),
            P("kv", None),
            P("req", None, "kv"),
            P("req", None, "kv"),
            P("req"),
            P("req", None),
            P("req", None),
            P("req", None),
            P(),
            P(None, ("req", "kv")),
            P(None, ("req", "kv")),
            P(None, ("req", "kv")),
        ),
        out_specs=(P("req", "kv"), P("req", None, "kv"), P("req", None, "kv")),
        check_vma=False,
    )
```

```python
import jax
import jax.numpy as jnp
from jax import lax
from jax.sharding import PartitionSpec as P

MIGP = 4


EPSILON = 1e-06
ROPE_BASE = 1000000.0


def rms_norm(values, scale_row):
    values = values.astype(jnp.float32)
    return (
        values * lax.rsqrt(jnp.mean(values * values, axis=-1, keepdims=True) + EPSILON) * scale_row
    )


def rotate(values, position):
    half_dim = values.shape[-1] // 2
    frequency = ROPE_BASE ** (-jnp.arange(half_dim, dtype=jnp.float32) * 2.0 / values.shape[-1])
    angles = position.astype(jnp.float32)[:, None, None] * frequency
    cosine = jnp.cos(angles)
    sine_part = jnp.sin(angles)
    first_half = values[..., :half_dim]
    second = values[..., half_dim:]
    return jnp.concatenate(
        [first_half * cosine - second * sine_part, second * cosine + first_half * sine_part],
        axis=-1,
    )


def attend_pool(queries, new_keys, new_values, k_pool, v_pool, lengths, page_table):
    req_count, kv_local, _, head_dim = queries.shape
    pool_pages, page_size, _ = k_pool.shape
    table_width = page_table.shape[1]
    token_count = pool_pages * page_size
    score_scale = head_dim ** (-0.5)
    slot_ids = jnp.arange(table_width, dtype=jnp.int32)
    in_use = slot_ids[None, :] < (lengths // page_size + 1)[:, None]
    match = (
        page_table[:, :, None] == jnp.arange(pool_pages, dtype=jnp.int32)[None, None, :]
    ) & in_use[:, :, None]
    page_mine = jnp.any(match, axis=1)
    page_start = jnp.sum(jnp.where(match, slot_ids[None, :, None] * page_size, 0), axis=1)
    token_pos = page_start[:, :, None] + jnp.arange(page_size, dtype=jnp.int32)[None, None, :]
    valid = (page_mine[:, :, None] & (token_pos < lengths[:, None, None])).reshape(
        req_count, token_count
    )
    keys = k_pool.reshape(token_count, kv_local, head_dim)
    values = v_pool.reshape(token_count, kv_local, head_dim)
    scores = (
        jnp.einsum("rkgd,tkd->rkgt", queries, keys, preferred_element_type=jnp.float32)
        * score_scale
    )
    scores = jnp.where(valid[:, None, None, :], scores, -jnp.inf)
    own_score = (
        jnp.einsum("rkgd,rkd->rkg", queries, new_keys, preferred_element_type=jnp.float32)
        * score_scale
    )
    row_top = jnp.maximum(jnp.max(scores, axis=-1), own_score)
    exps_all = jnp.exp(scores - row_top[..., None])
    own_exp = jnp.exp(own_score - row_top)
    denom_sum = jnp.sum(exps_all, axis=-1) + own_exp
    weights = (exps_all / denom_sum[..., None]).astype(jnp.bfloat16)
    own_weight = (own_exp / denom_sum).astype(jnp.bfloat16)
    start_sum = jnp.einsum(
        "rkg,rkd->rkgd", own_weight, new_values, preferred_element_type=jnp.float32
    )
    return start_sum + jnp.einsum(
        "rkgt,tkd->rkgd", weights, values, preferred_element_type=jnp.float32
    )


def sum_from_peers(pieces, axis):
    count = lax.axis_size(axis)
    me = lax.axis_index(axis)
    total = pieces[me]
    for shift in range(1, count):
        total = total + lax.ppermute(
            pieces[(me + shift) % count], axis, [(k, (k + shift) % count) for k in range(count)]
        )
    return total


def layer_body(
    hidden,
    attn_gain,
    q_gain,
    k_gain,
    w_q,
    w_gate_attn,
    w_k,
    w_v,
    w_o,
    k_pool,
    v_pool,
    lengths,
    page_table,
    mig_request,
    mig_dest,
    mlp_gain,
    w_gate,
    w_up,
    w_down,
):
    head_dim = q_gain.shape[0]
    req_count = hidden.shape[0]
    kv_local = w_k.shape[1] // head_dim
    q_local = w_q.shape[1] // head_dim
    group_size = q_local // kv_local
    page_size = k_pool.shape[1]
    channels = kv_local * head_dim
    model_width = mlp_gain.shape[0]
    unit_count = w_gate.shape[1]
    stacked = lax.all_gather(
        jnp.concatenate([w_gate.T, w_up.T, w_down.T], axis=0), "kv", axis=0, tiled=False
    )
    gate_w = stacked[:, :unit_count, :]
    up_w = stacked[:, unit_count : 2 * unit_count, :]
    down_w = stacked[:, 2 * unit_count :, :]
    whole_rows = lax.all_gather(hidden, "kv", axis=1, tiled=True)
    normed = rms_norm(whole_rows, attn_gain).astype(jnp.bfloat16)
    query_raw = jnp.dot(normed, w_q, preferred_element_type=jnp.float32).reshape(
        req_count, q_local, head_dim
    )
    gate_raw = jnp.dot(normed, w_gate_attn, preferred_element_type=jnp.float32)
    key_raw = jnp.dot(normed, w_k, preferred_element_type=jnp.float32).reshape(
        req_count, kv_local, head_dim
    )
    value_raw = jnp.dot(normed, w_v, preferred_element_type=jnp.float32).reshape(
        req_count, kv_local, head_dim
    )
    queries = rotate(rms_norm(query_raw, q_gain), lengths).astype(jnp.bfloat16)
    queries = queries.reshape(req_count, kv_local, group_size, head_dim)
    new_keys = rotate(rms_norm(key_raw, k_gain), lengths).astype(jnp.bfloat16)
    new_values = value_raw.astype(jnp.bfloat16)
    mig_rows = mig_request[0]
    dest_row = mig_dest[0]
    mig_count = mig_rows.shape[0]
    slot_count = MIGP * page_size
    inverse = jnp.zeros_like(dest_row).at[dest_row].set(jnp.arange(mig_count, dtype=jnp.int32))
    sent_rows = mig_rows[inverse]
    moved_pages = page_table[sent_rows, :MIGP]
    slot_pos = jnp.arange(slot_count, dtype=jnp.int32)[None, :, None]
    moved_len = lengths[sent_rows][:, None, None]
    zero_value = jnp.zeros((), jnp.bfloat16)

    def place_cache(pool, fresh_rows):
        cached = pool[moved_pages].reshape(mig_count, slot_count, channels)
        fresh_row = fresh_rows.reshape(req_count, channels)[sent_rows][:, None, :]
        return jnp.where(
            slot_pos < moved_len, cached, jnp.where(slot_pos == moved_len, fresh_row, zero_value)
        )

    moving = lax.all_to_all(
        jnp.stack([place_cache(k_pool, new_keys), place_cache(v_pool, new_values)], axis=1),
        "req",
        0,
        0,
        tiled=True,
    )
    mig_keys = moving[:, 0]
    mig_values = moving[:, 1]
    context = attend_pool(queries, new_keys, new_values, k_pool, v_pool, lengths, page_table)
    gated = (jax.nn.sigmoid(gate_raw) * context.reshape(req_count, q_local * head_dim)).astype(
        jnp.bfloat16
    )
    head_terms = jnp.dot(gated, w_o, preferred_element_type=jnp.float32)
    kv_count = lax.axis_size("kv")
    req_groups = lax.axis_size("req")
    slice_width = model_width // kv_count
    row_share = req_count // kv_count
    kv_index = lax.axis_index("kv")
    attn_rows = sum_from_peers(head_terms.reshape(kv_count, row_share, model_width), "kv")
    own_rows = lax.dynamic_slice_in_dim(whole_rows, kv_index * row_share, row_share, 0)
    mid_rows = (own_rows.astype(jnp.float32) + attn_rows).astype(jnp.bfloat16)
    normed_rows = rms_norm(mid_rows, mlp_gain).astype(jnp.bfloat16)
    row_block = lax.all_gather(normed_rows, "req", axis=0, tiled=True)
    gate_part = jnp.einsum("nd,sud->nsu", row_block, gate_w, preferred_element_type=jnp.float32)
    up_part = jnp.einsum("nd,sud->nsu", row_block, up_w, preferred_element_type=jnp.float32)
    activation = (jax.nn.silu(gate_part) * up_part).astype(jnp.bfloat16)
    down_part = jnp.einsum(
        "nsu,suc->nc", activation, down_w, preferred_element_type=jnp.float32
    )
    mlp_rows = sum_from_peers(down_part.reshape(req_groups, row_share, model_width), "req")
    out_rows = (mid_rows.astype(jnp.float32) + mlp_rows).astype(jnp.bfloat16)
    col_pieces = out_rows.reshape(row_share, kv_count, slice_width).transpose(1, 0, 2)
    by_shift = [col_pieces[kv_index]]
    for shift in range(1, kv_count):
        by_shift.append(
            lax.ppermute(
                col_pieces[(kv_index + shift) % kv_count],
                "kv",
                [(k, (k + shift) % kv_count) for k in range(kv_count)],
            )
        )
    by_shift = jnp.stack(by_shift, axis=0)
    sources = (kv_index - jnp.arange(kv_count, dtype=jnp.int32)) % kv_count
    out_hidden = by_shift[sources].reshape(kv_count * row_share, slice_width)
    return (out_hidden, mig_keys, mig_values)


def solution(mesh):
    return jax.shard_map(
        layer_body,
        mesh=mesh,
        in_specs=(
            P("req", "kv"),
            P(),
            P(),
            P(),
            P(None, "kv"),
            P(None, "kv"),
            P(None, "kv"),
            P(None, "kv"),
            P("kv", None),
            P("req", None, "kv"),
            P("req", None, "kv"),
            P("req"),
            P("req", None),
            P("req", None),
            P("req", None),
            P(),
            P(None, ("req", "kv")),
            P(None, ("req", "kv")),
            P(None, ("req", "kv")),
        ),
        out_specs=(P("req", "kv"), P("req", None, "kv"), P("req", None, "kv")),
        check_vma=False,
    )
```

```python
import jax
import jax.numpy as jnp
from jax import lax
from jax.sharding import PartitionSpec as P

MIGP = 4


EPSILON = 1e-06
ROPE_BASE = 1000000.0


def rms_norm(values, scale_row):
    values = values.astype(jnp.float32)
    return (
        values * lax.rsqrt(jnp.mean(values * values, axis=-1, keepdims=True) + EPSILON) * scale_row
    )


def rotate(values, position):
    half_dim = values.shape[-1] // 2
    frequency = ROPE_BASE ** (-jnp.arange(half_dim, dtype=jnp.float32) * 2.0 / values.shape[-1])
    angles = position.astype(jnp.float32)[:, None, None] * frequency
    cosine = jnp.cos(angles)
    sine_part = jnp.sin(angles)
    first_half = values[..., :half_dim]
    second = values[..., half_dim:]
    return jnp.concatenate(
        [first_half * cosine - second * sine_part, second * cosine + first_half * sine_part],
        axis=-1,
    )


def attend_pool(queries, new_keys, new_values, k_pool, v_pool, lengths, page_table):
    req_count, kv_local, _, head_dim = queries.shape
    pool_pages, page_size, _ = k_pool.shape
    table_width = page_table.shape[1]
    token_count = pool_pages * page_size
    score_scale = head_dim ** (-0.5)
    slot_ids = jnp.arange(table_width, dtype=jnp.int32)
    in_use = slot_ids[None, :] < (lengths // page_size + 1)[:, None]
    match = (
        page_table[:, :, None] == jnp.arange(pool_pages, dtype=jnp.int32)[None, None, :]
    ) & in_use[:, :, None]
    page_mine = jnp.any(match, axis=1)
    page_start = jnp.sum(jnp.where(match, slot_ids[None, :, None] * page_size, 0), axis=1)
    token_pos = page_start[:, :, None] + jnp.arange(page_size, dtype=jnp.int32)[None, None, :]
    valid = (page_mine[:, :, None] & (token_pos < lengths[:, None, None])).reshape(
        req_count, token_count
    )
    keys = k_pool.reshape(token_count, kv_local, head_dim)
    values = v_pool.reshape(token_count, kv_local, head_dim)
    scores = (
        jnp.einsum("rkgd,tkd->rkgt", queries, keys, preferred_element_type=jnp.float32)
        * score_scale
    )
    scores = jnp.where(valid[:, None, None, :], scores, -jnp.inf)
    own_score = (
        jnp.einsum("rkgd,rkd->rkg", queries, new_keys, preferred_element_type=jnp.float32)
        * score_scale
    )
    row_top = jnp.maximum(jnp.max(scores, axis=-1), own_score)
    exps_all = jnp.exp(scores - row_top[..., None])
    own_exp = jnp.exp(own_score - row_top)
    denom_sum = jnp.sum(exps_all, axis=-1) + own_exp
    weights = (exps_all / denom_sum[..., None]).astype(jnp.bfloat16)
    own_weight = (own_exp / denom_sum).astype(jnp.bfloat16)
    start_sum = jnp.einsum(
        "rkg,rkd->rkgd", own_weight, new_values, preferred_element_type=jnp.float32
    )
    return start_sum + jnp.einsum(
        "rkgt,tkd->rkgd", weights, values, preferred_element_type=jnp.float32
    )


def reduce_to_slice(partial, kv_count, slice_width):
    rows = partial.shape[0]
    pieces = partial.reshape(rows, kv_count, slice_width).transpose(1, 0, 2)
    arrived = lax.all_to_all(pieces, "kv", 0, 0, tiled=True)
    return jnp.sum(arrived, axis=0)


def reduce_by_permutes(partial, kv_count, slice_width):
    rows = partial.shape[0]
    pieces = partial.reshape(rows, kv_count, slice_width).transpose(1, 0, 2)
    me = lax.axis_index("kv")
    total = pieces[me]
    for shift in range(1, kv_count):
        total = total + lax.ppermute(
            pieces[(me + shift) % kv_count],
            "kv",
            [(k, (k + shift) % kv_count) for k in range(kv_count)],
        )
    return total


def layer_body(
    hidden,
    attn_gain,
    q_gain,
    k_gain,
    w_q,
    w_gate_attn,
    w_k,
    w_v,
    w_o,
    k_pool,
    v_pool,
    lengths,
    page_table,
    mig_request,
    mig_dest,
    mlp_gain,
    w_gate,
    w_up,
    w_down,
):
    head_dim = q_gain.shape[0]
    req_count = hidden.shape[0]
    kv_local = w_k.shape[1] // head_dim
    q_local = w_q.shape[1] // head_dim
    group_size = q_local // kv_local
    page_size = k_pool.shape[1]
    channels = kv_local * head_dim
    model_width = mlp_gain.shape[0]
    unit_count = w_gate.shape[1]
    stacked = lax.all_gather(
        jnp.concatenate([w_gate.T, w_up.T, w_down.T], axis=0), "req", axis=0, tiled=False
    )
    gate_w = stacked[:, :unit_count, :]
    up_w = stacked[:, unit_count : 2 * unit_count, :]
    down_w = stacked[:, 2 * unit_count :, :]
    whole_rows = lax.all_gather(hidden, "kv", axis=1, tiled=True)
    normed = rms_norm(whole_rows, attn_gain).astype(jnp.bfloat16)
    query_raw = jnp.dot(normed, w_q, preferred_element_type=jnp.float32).reshape(
        req_count, q_local, head_dim
    )
    gate_raw = jnp.dot(normed, w_gate_attn, preferred_element_type=jnp.float32)
    key_raw = jnp.dot(normed, w_k, preferred_element_type=jnp.float32).reshape(
        req_count, kv_local, head_dim
    )
    value_raw = jnp.dot(normed, w_v, preferred_element_type=jnp.float32).reshape(
        req_count, kv_local, head_dim
    )
    queries = rotate(rms_norm(query_raw, q_gain), lengths).astype(jnp.bfloat16)
    queries = queries.reshape(req_count, kv_local, group_size, head_dim)
    new_keys = rotate(rms_norm(key_raw, k_gain), lengths).astype(jnp.bfloat16)
    new_values = value_raw.astype(jnp.bfloat16)
    mig_rows = mig_request[0]
    dest_row = mig_dest[0]
    mig_count = mig_rows.shape[0]
    slot_count = MIGP * page_size
    inverse = jnp.zeros_like(dest_row).at[dest_row].set(jnp.arange(mig_count, dtype=jnp.int32))
    sent_rows = mig_rows[inverse]
    moved_pages = page_table[sent_rows, :MIGP]
    slot_pos = jnp.arange(slot_count, dtype=jnp.int32)[None, :, None]
    moved_len = lengths[sent_rows][:, None, None]
    zero_value = jnp.zeros((), jnp.bfloat16)

    def place_cache(pool, fresh_rows):
        cached = pool[moved_pages].reshape(mig_count, slot_count, channels)
        fresh_row = fresh_rows.reshape(req_count, channels)[sent_rows][:, None, :]
        return jnp.where(
            slot_pos < moved_len, cached, jnp.where(slot_pos == moved_len, fresh_row, zero_value)
        )

    mig_keys = lax.all_to_all(place_cache(k_pool, new_keys), "req", 0, 0, tiled=True)
    mig_values = lax.all_to_all(place_cache(v_pool, new_values), "req", 0, 0, tiled=True)
    context = attend_pool(queries, new_keys, new_values, k_pool, v_pool, lengths, page_table)
    gated = (jax.nn.sigmoid(gate_raw) * context.reshape(req_count, q_local * head_dim)).astype(
        jnp.bfloat16
    )
    head_terms = jnp.dot(gated, w_o, preferred_element_type=jnp.float32)
    kv_count = lax.axis_size("kv")
    slice_width = model_width // kv_count
    mid_slice = (
        hidden.astype(jnp.float32) + reduce_to_slice(head_terms, kv_count, slice_width)
    ).astype(jnp.bfloat16)
    mid_stream = lax.all_gather(mid_slice, "kv", axis=1, tiled=True)
    normed_mlp = rms_norm(mid_stream, mlp_gain).astype(jnp.bfloat16)
    gate_part = jnp.einsum("rd,sud->rsu", normed_mlp, gate_w, preferred_element_type=jnp.float32)
    up_part = jnp.einsum("rd,sud->rsu", normed_mlp, up_w, preferred_element_type=jnp.float32)
    activation = (jax.nn.silu(gate_part) * up_part).astype(jnp.bfloat16)
    down_part = jnp.einsum("rsu,suc->rc", activation, down_w, preferred_element_type=jnp.float32)
    mlp_part = reduce_by_permutes(down_part, kv_count, slice_width)
    out_hidden = (mid_slice.astype(jnp.float32) + mlp_part).astype(jnp.bfloat16)
    return (out_hidden, mig_keys, mig_values)


def solution(mesh):
    return jax.shard_map(
        layer_body,
        mesh=mesh,
        in_specs=(
            P("req", "kv"),
            P(),
            P(),
            P(),
            P(None, "kv"),
            P(None, "kv"),
            P(None, "kv"),
            P(None, "kv"),
            P("kv", None),
            P("req", None, "kv"),
            P("req", None, "kv"),
            P("req"),
            P("req", None),
            P("req", None),
            P("req", None),
            P(),
            P(None, ("req", "kv")),
            P(None, ("req", "kv")),
            P(None, ("req", "kv")),
        ),
        out_specs=(P("req", "kv"), P("req", None, "kv"), P("req", None, "kv")),
        check_vma=False,
    )
```
